512 devices in a mesh: section: 2 (over x_lo), seq: 64 (over y, z), tp: 4 (over x_hi, core).
Axes of the slice: x: 4 (x_hi: 2, x_lo: 2; x = x_hi * 2 + x_lo), y: 8, z: 8, core: 2. Of those that a mesh axis runs over, the one named last changes fastest.
Arguments:
- tokens: bfloat16 [2, 4096, 1536], P(None, 'seq', 'tp')
- input_weight: bfloat16 [2, 1536, 3, 1024], P('section', None, None, 'tp')
- output_weight: bfloat16 [2, 1024, 1536], P('section', 'tp'), may hold values from -0.1875 to 0.1875
- modulation: float32 [2, 3, 1536], P('section'), may hold values from -3 to 3
- norm_gain: float32 [2, 2, 1024], P('section', None, 'tp'), may hold values from 1.2 to 2.5
- stale_cache: bfloat16 [2, 2, 2, 4096, 1024], P('section', None, None, 'seq', 'tp'), as said below
- recompute: int32 [2, 2, 256], P('section'), may hold values from 0 to 63, as said below
- positions: int32 [3, 2, 4096], P(None, None, 'seq'), may hold values from 0 to 66
- lengths: int32 [2], replicated, may hold values from 2048 to 4096, as said below
Outputs:
- layer_outputs: bfloat16 [2, 2, 4096, 1536], P('section', None, 'seq', 'tp')
The draws below stay inside these ranges and needn't reach their ends.
Inputs may be any that keep to these rules, and one draw needn't show every extreme that they name: `stale_cache`: the keys already carry their rotary turn. `recompute`: each aligned block of 4 entries belongs to one patch, in patch order, and names distinct rows of that patch. `lengths`: an item's live slots are its first ones; at least half of the 4096 slots are live, and in every draw one item fills all of them.
All inputs are finite; a program needn't handle non-finite values.
Results may differ from the reference program's by a relative error of at most 0.02.
Values may be sent and summed in bfloat16 or wider, within the bound.
No kernel may reach another device: no remote copies, remote signals or barrier semaphores. Data moves between devices by JAX's collectives and lax.ppermute only.
A program may use at most 64 MiB of HBM per device.

```python
import math
import jax
import jax.numpy as jnp
from jax import lax

D = 1536
HD = 128
HEADS = 8
ITEMS = 2
TOK_DEV = 64
LAYERS = 2
TOKENS = 4096
RECOMP = 4


def draw_tokens(key, part):
    pieces = jax.random.split(key, 3)
    shape_all = (ITEMS, TOKENS, D)
    base_values = jnp.clip(jax.random.normal(pieces[0], shape_all), -4.0, 4.0)
    row_scale = jnp.exp(jax.random.uniform(pieces[1], (ITEMS, TOKENS, 1), minval=jnp.log(0.3), maxval=jnp.log(3.0)))
    column_scale = jnp.exp(jax.random.uniform(pieces[2], (1, 1, D), minval=jnp.log(0.3), maxval=jnp.log(3.0)))
    return (base_values * row_scale * column_scale).astype(jnp.bfloat16)


def draw_input_weight(key, part):
    head_width = HEADS * HD
    shape_all = (LAYERS, D, 3, head_width)
    ramp_values = jnp.arange(head_width, dtype=jnp.float32) / (head_width - 1) - 0.5
    base_values = jnp.clip(jax.random.normal(key, shape_all), -4.0, 4.0)
    factor = 3.0
    column_scale = jnp.exp(jnp.log(factor) * ramp_values) * D ** (-0.5)
    return (base_values * column_scale).astype(jnp.bfloat16)


def draw_stale_cache(key, part):
    head_width = HEADS * HD
    shape_half = (LAYERS, ITEMS, TOKENS, head_width)
    pieces = jax.random.split(key, 2)
    key_part = jnp.clip(jax.random.normal(pieces[0], shape_half), -4.0, 4.0) * 1.7
    value_part = jnp.clip(jax.random.normal(pieces[1], shape_half), -4.0, 4.0)
    return jnp.stack([key_part, value_part], axis=2).astype(jnp.bfloat16)


def draw_recompute(key, part):
    patch_count = TOKENS // TOK_DEV
    subkeys = jax.random.split(key, LAYERS * ITEMS * patch_count)
    picked = jax.vmap(lambda subkey: jax.random.permutation(subkey, TOK_DEV)[:RECOMP])(subkeys)
    return picked.reshape(LAYERS, ITEMS, patch_count * RECOMP).astype(jnp.int32)


def draw_positions(key, part):
    pieces = jax.random.split(key, 7)
    item_number = jnp.arange(ITEMS, dtype=jnp.int32)[:, None]
    first_item = jax.random.randint(pieces[6], (), 0, ITEMS)
    second_item = (first_item + 1) % ITEMS
    width_cells = jax.random.randint(pieces[0], (ITEMS, 1), 8, 33)
    height_cells = jax.random.randint(pieces[1], (ITEMS, 1), 8, 17)
    offset = jax.random.randint(pieces[2], (ITEMS, 1), 0, 4)
    width_shift = jax.random.randint(pieces[3], (ITEMS, 1), 0, 25)
    height_shift = jax.random.randint(pieces[4], (ITEMS, 1), 0, 9)
    second_height_shift = jax.random.randint(pieces[5], (ITEMS, 1), 0, 17)
    is_first = item_number == first_item
    is_second = item_number == second_item
    width_cells = jnp.where(is_first, 32, jnp.where(is_second, 8, width_cells))
    height_cells = jnp.where(is_second, 8, height_cells)
    offset = jnp.where(is_second, 3, offset)
    width_shift = jnp.where(is_first, 0, jnp.minimum(width_shift, 32 - width_cells))
    height_shift = jnp.where(is_first, 0, jnp.where(is_second, second_height_shift, height_shift))
    slot_number = jnp.arange(TOKENS, dtype=jnp.int32)[None, :]
    frame_index = slot_number // (width_cells * height_cells) + offset
    height_index = slot_number // width_cells % height_cells + height_shift
    width_index = slot_number % width_cells + width_shift
    return jnp.stack([frame_index, height_index, width_index]).astype(jnp.int32)


def draw_lengths(key, part):
    pieces = jax.random.split(key, 2)
    drawn = jax.random.randint(pieces[0], (ITEMS,), TOKENS // 2, TOKENS + 1)
    fullest = jax.random.randint(pieces[1], (), 0, ITEMS)
    return jnp.where(jnp.arange(ITEMS) == fullest, TOKENS, drawn).astype(jnp.int32)


def block_scale(own_key, extent, cuts, smallest, largest):
    def one(position, shards_of):
        steps = jax.random.uniform(jax.random.fold_in(jax.random.fold_in(own_key, 6), position), (shards_of,), jnp.float32, smallest / len(cuts), largest / len(cuts))
        return jnp.repeat(jnp.exp(steps), extent[position] // shards_of).reshape((-1,) + (1,) * (len(extent) - position - 1))

    factor_of = one(*cuts[0])
    for cut in cuts[1:]:
        factor_of = factor_of * one(*cut)
    return factor_of


def bell_draw(rng, extent, width, most, cuts=(), held_as=jnp.bfloat16):
    loudness = block_scale(rng, extent, cuts, -0.22, 0.18) if cuts else 1.0
    values = jax.random.normal(rng, extent, jnp.float32) * width * loudness
    return jnp.minimum(jnp.maximum(values, -most), most).astype(held_as)


def setup_inputs(seed: int = 0) -> dict:
    key_list = jax.random.split(jax.random.key(seed), 10)
    return {
        "tokens": draw_tokens(jax.random.fold_in(key_list[9], 71), 0),
        "input_weight": draw_input_weight(jax.random.fold_in(key_list[9], 71), 0),
        "output_weight": bell_draw(key_list[2], (LAYERS, HEADS * HD, D), (HEADS * HD) ** -0.5, 0.1875, ((0, 2), (1, 4))),
        "modulation": bell_draw(key_list[3], (LAYERS, 3, D), 0.6, 3.0, ((0, 2),), jnp.float32),
        "norm_gain": jnp.clip(jnp.exp(math.log(2.5) - 0.73396914 * jax.random.uniform(key_list[4], (LAYERS, 2, HEADS * HD), jnp.float32) ** block_scale(key_list[4], (LAYERS, 2, HEADS * HD), ((0, 2), (2, 4)), -0.2, 0.2)), 1.2, 2.5),
        "stale_cache": draw_stale_cache(jax.random.fold_in(key_list[9], 71), 0),
        "recompute": draw_recompute(jax.random.fold_in(key_list[9], 71), 0),
        "positions": draw_positions(jax.random.fold_in(key_list[9], 71), 0),
        "lengths": draw_lengths(jax.random.fold_in(key_list[9], 71), 0),
    }


floor_score = -1e+30

def rotate(field_rows, frame_place, height_place, width_place):
    row_count = field_rows.shape[0]
    pair_count = HD // 2
    side_pairs = pair_count // 3
    frame_pairs = pair_count - 2 * side_pairs

    def spacing(pair_total):
        ladder = jnp.arange(pair_total, dtype=jnp.float32)
        return jnp.power(jnp.float32(10000.0), -ladder / pair_total)
    angles = jnp.concatenate([frame_place.astype(jnp.float32)[:, None] * spacing(frame_pairs)[None, :], height_place.astype(jnp.float32)[:, None] * spacing(side_pairs)[None, :], width_place.astype(jnp.float32)[:, None] * spacing(side_pairs)[None, :]], axis=1)
    cosine = jnp.cos(angles)[:, None, :]
    sine_part = jnp.sin(angles)[:, None, :]
    paired = field_rows.reshape(row_count, -1, pair_count, 2)
    first_half = paired[..., 0]
    second = paired[..., 1]
    turned = jnp.stack([first_half * cosine - second * sine_part, first_half * sine_part + second * cosine], axis=-1)
    return turned.reshape(row_count, -1)

def layer_apply(layer_in, joint_weight, out_weight, modulate_rows, norm_gains, stale_pair, chosen, item_places, length):
    head_width = HEADS * HD
    patch_count = TOKENS // TOK_DEV
    slot_number = jnp.arange(TOKENS, dtype=jnp.int32)
    as_float = layer_in.astype(jnp.float32)
    row_mean = lax.optimization_barrier(jnp.mean(as_float, axis=-1, keepdims=True))
    centered = as_float - row_mean
    variance = lax.optimization_barrier(jnp.mean(centered * centered, axis=-1, keepdims=True))
    modulated = (centered * lax.rsqrt(variance + 1e-06) * (1.0 + modulate_rows[1]) + modulate_rows[0]).astype(jnp.bfloat16)
    projected = jnp.dot(modulated, joint_weight.reshape(D, 3 * head_width), preferred_element_type=jnp.float32).reshape(TOKENS, 3, head_width)
    query_raw = projected[:, 0]
    key_raw = projected[:, 1]
    value_rows = projected[:, 2].astype(jnp.bfloat16)
    query_normed = query_raw * lax.rsqrt(lax.optimization_barrier(jnp.mean(query_raw * query_raw, axis=-1, keepdims=True)) + 1e-06) * norm_gains[0]
    key_normed = key_raw * lax.rsqrt(lax.optimization_barrier(jnp.mean(key_raw * key_raw, axis=-1, keepdims=True)) + 1e-06) * norm_gains[1]
    fresh_query = rotate(query_normed, item_places[0], item_places[1], item_places[2]).astype(jnp.bfloat16)
    fresh_key = rotate(key_normed, item_places[0], item_places[1], item_places[2]).astype(jnp.bfloat16)
    chosen_slots = (jnp.arange(patch_count, dtype=jnp.int32)[:, None] * TOK_DEV + chosen.reshape(patch_count, RECOMP).astype(jnp.int32)).reshape(-1)
    refreshed = jnp.zeros((TOKENS,), dtype=bool).at[chosen_slots].set(True)
    mixed_key = jnp.where(refreshed[:, None], fresh_key, stale_pair[0])
    mixed_value = jnp.where(refreshed[:, None], value_rows, stale_pair[1])
    valid_slots = slot_number < length

    def patch_attention(patch_number):
        first_slot = (patch_number * TOK_DEV).astype(jnp.int32)
        key_rows = lax.dynamic_update_slice_in_dim(mixed_key, lax.dynamic_slice_in_dim(fresh_key, first_slot, TOK_DEV, 0), first_slot, 0)
        value_block = lax.dynamic_update_slice_in_dim(mixed_value, lax.dynamic_slice_in_dim(value_rows, first_slot, TOK_DEV, 0), first_slot, 0)
        query_rows = lax.dynamic_slice_in_dim(fresh_query, first_slot, TOK_DEV, 0)
        query_heads = query_rows.astype(jnp.float32).reshape(TOK_DEV, HEADS, HD)
        key_heads = key_rows.astype(jnp.float32).reshape(TOKENS, HEADS, HD)
        value_heads = value_block.astype(jnp.float32).reshape(TOKENS, HEADS, HD)
        scores = jnp.einsum('rhd,khd->hrk', query_heads, key_heads) * HD ** (-0.5)
        scores = jnp.where(valid_slots[None, None, :], scores, floor_score)
        top_score = lax.optimization_barrier(jnp.max(scores, axis=-1, keepdims=True))
        probability = jnp.where(valid_slots[None, None, :], jnp.exp(scores - top_score), 0.0)
        denominator = lax.optimization_barrier(jnp.sum(probability, axis=-1))
        rounded = lax.optimization_barrier(probability.astype(jnp.bfloat16))
        numerator = jnp.einsum('hrk,khd->hrd', rounded.astype(jnp.float32), value_heads)
        return (numerator / denominator[..., None]).transpose(1, 0, 2).reshape(TOK_DEV, head_width).astype(jnp.bfloat16)
    attention = lax.map(patch_attention, jnp.arange(patch_count, dtype=jnp.int32)).reshape(TOKENS, head_width)
    projected_out = jnp.dot(attention, out_weight, preferred_element_type=jnp.float32)
    result = as_float + modulate_rows[2] * projected_out
    return jnp.where(valid_slots[:, None], result, 0.0).astype(jnp.bfloat16)

def reference(tokens, input_weight, output_weight, modulation, norm_gain, stale_cache, recompute, positions, lengths):
    collected = [[] for layer_number in range(LAYERS)]
    for item_number in range(ITEMS):
        carried = tokens[item_number]
        for layer_number in range(LAYERS):
            carried = layer_apply(carried, input_weight[layer_number], output_weight[layer_number], modulation[layer_number], norm_gain[layer_number], stale_cache[layer_number, item_number], recompute[layer_number, item_number], positions[:, item_number], lengths[item_number])
            collected[layer_number].append(carried)
    return jnp.stack([jnp.stack(layer_list) for layer_list in collected])
```

```python
import jax
import jax.numpy as jnp
from jax import lax
from jax.sharding import PartitionSpec as P

HD = 128
RECOMP = 4
RING = 8


floor_score = -1e30


def shift_perm(count, step, inner):
    pairs = []
    for s in range(count):
        if inner == 1:
            outer, pos = divmod(s, RING)
            pairs.append((s, ((outer + step) % RING) * RING + pos))
        else:
            outer, pos = divmod(s, RING)
            pairs.append((s, outer * RING + (pos + step) % RING))
    return pairs


def ring_gather(block, count, along_z):
    inner = RING if along_z else 1
    plus = shift_perm(count, 1, inner)
    minus = shift_perm(count, -1, inner)
    rel = [None] * RING
    rel[0] = block
    fwd = block
    bwd = block
    for step in range(1, RING // 2):
        fwd = lax.ppermute(fwd, "seq", plus)
        bwd = lax.ppermute(bwd, "seq", minus)
        rel[RING - step] = fwd
        rel[step] = bwd
    rel[RING // 2] = lax.ppermute(fwd, "seq", plus)
    return jnp.stack(rel)


def gather_2d(block, count, z_first):
    first = ring_gather(block, count, along_z=z_first)
    return ring_gather(first, count, along_z=not z_first)


def tp_parts(x):
    n = lax.axis_size("tp")
    parts = [x]
    for d in range(1, n):
        parts.append(lax.ppermute(x, "tp", [(i, (i + d) % n) for i in range(n)]))
    return parts


def rotate(field_rows, frame_place, height_place, width_place):
    lead = field_rows.shape[:-1]
    pair_count = HD // 2
    side_pairs = pair_count // 3
    frame_pairs = pair_count - 2 * side_pairs

    def spacing(pair_total):
        ladder = jnp.arange(pair_total, dtype=jnp.float32)
        return jnp.power(jnp.float32(10000.0), -ladder / pair_total)

    angles = jnp.concatenate(
        [
            frame_place.astype(jnp.float32)[..., None] * spacing(frame_pairs),
            height_place.astype(jnp.float32)[..., None] * spacing(side_pairs),
            width_place.astype(jnp.float32)[..., None] * spacing(side_pairs),
        ],
        axis=-1,
    )
    cosine = jnp.cos(angles)[..., None, :]
    sine_part = jnp.sin(angles)[..., None, :]
    paired = field_rows.reshape(lead + (-1, pair_count, 2))
    first_half = paired[..., 0]
    second = paired[..., 1]
    turned = jnp.stack(
        [first_half * cosine - second * sine_part, first_half * sine_part + second * cosine],
        axis=-1,
    )
    return turned.reshape(lead + (-1,))


def attend(query, keys, values, keep):
    scores = jnp.einsum(
        "iqd,abikd->iqabk", query, keys, preferred_element_type=jnp.float32
    ) * HD ** (-0.5)
    mask = jnp.transpose(keep, (2, 0, 1, 3))[:, None]
    scores = jnp.where(mask, scores, floor_score)
    top = jnp.max(scores, axis=(2, 3, 4), keepdims=True)
    weights = jnp.where(mask, jnp.exp(scores - top), 0.0)
    total = jnp.sum(weights, axis=(2, 3, 4))
    numerator = jnp.einsum(
        "iqabk,abikd->iqd", weights.astype(jnp.bfloat16), values, preferred_element_type=jnp.float32
    )
    return numerator / total[..., None]


def local(
    tokens,
    input_weight,
    output_weight,
    modulation,
    norm_gain,
    stale_cache,
    recompute,
    positions,
    lengths,
):
    section_index = lax.axis_index("section")
    seq_count = lax.axis_size("seq")
    patch_index = lax.axis_index("seq")
    split_count = lax.axis_size("tp")
    split_index = lax.axis_index("tp")
    item_count = tokens.shape[0]
    local_rows = tokens.shape[1]
    feature_shard = tokens.shape[2]
    feature_total = feature_shard * split_count
    head_width = input_weight.shape[3]
    joint_weight = input_weight[0].reshape(feature_total, 3 * head_width)
    out_weight = output_weight[0]
    modulate_rows = modulation[0]
    norm_gains = norm_gain[0]
    gate_shard = lax.dynamic_slice_in_dim(
        modulate_rows[2], split_index * feature_shard, feature_shard
    )
    row_y = patch_index // RING
    row_z = patch_index % RING
    local_number = jnp.arange(local_rows, dtype=jnp.int32)
    row_slots = patch_index * local_rows + local_number

    stale = stale_cache[0]
    stale_a = gather_2d(stale[..., :HD], seq_count, z_first=True)
    stale_b = gather_2d(stale[..., HD:], seq_count, z_first=False)

    ring_offsets = jnp.arange(RING, dtype=jnp.int32)
    patch_a = ((row_y + ring_offsets[:, None]) % RING) * RING + (row_z + ring_offsets[None, :]) % RING
    patch_b = ((row_y + ring_offsets[None, :]) % RING) * RING + (row_z + ring_offsets[:, None]) % RING
    chosen_all = recompute[0].reshape(item_count, seq_count, RECOMP)
    own_block = (ring_offsets[:, None] == 0) & (ring_offsets[None, :] == 0)

    def block_tables(patch_of):
        picks = jnp.take(chosen_all, patch_of.reshape(-1), axis=1).reshape(
            item_count, RING, RING, RECOMP
        )
        picks = jnp.transpose(picks, (1, 2, 0, 3))
        slots = patch_of[:, :, None, None] * local_rows + local_number
        keep = slots < lengths[None, None, :, None]
        return picks, keep

    picks_a, keep_a = block_tables(patch_a)
    picks_b, keep_b = block_tables(patch_b)
    own_chosen = lax.dynamic_slice_in_dim(chosen_all, patch_index, 1, axis=1)[:, 0]

    def mixed(stale_full, fresh_full, own_fresh, picks):
        out = stale_full
        for r in range(RECOMP):
            hit = local_number[None, None, None, None, :] == picks[:, :, :, None, r : r + 1]
            out = jnp.where(hit[..., None], fresh_full[:, :, :, :, r : r + 1, :], out)
        out = jnp.where(own_block[:, :, None, None, None, None], own_fresh[None, None], out)
        return out

    def layer(layer_in):
        parts = tp_parts(layer_in)
        gathered = jnp.zeros((item_count, local_rows, feature_total), layer_in.dtype)
        for d, part in enumerate(parts):
            owner = (split_index - d) % split_count
            gathered = lax.dynamic_update_slice_in_dim(gathered, part, owner * feature_shard, axis=2)
        as_float = gathered.astype(jnp.float32)
        row_mean = jnp.mean(as_float, axis=-1, keepdims=True)
        centered = as_float - row_mean
        variance = jnp.mean(centered * centered, axis=-1, keepdims=True)
        modulated = (
            centered * lax.rsqrt(variance + 1e-06) * (1.0 + modulate_rows[1]) + modulate_rows[0]
        ).astype(jnp.bfloat16)
        projected = jnp.dot(modulated, joint_weight, preferred_element_type=jnp.float32).reshape(
            item_count, local_rows, 3, head_width
        )
        query_raw = projected[:, :, 0]
        key_raw = projected[:, :, 1]
        value_rows = projected[:, :, 2].astype(jnp.bfloat16)
        squares = jnp.stack(
            [jnp.sum(query_raw * query_raw, axis=-1), jnp.sum(key_raw * key_raw, axis=-1)]
        )
        square_parts = tp_parts(squares)
        square_total = square_parts[0]
        for part in square_parts[1:]:
            square_total = square_total + part
        entry_total = head_width * split_count
        query_normed = (
            query_raw * lax.rsqrt(square_total[0] / entry_total + 1e-06)[..., None] * norm_gains[0]
        )
        key_normed = key_raw * lax.rsqrt(square_total[1] / entry_total + 1e-06)[..., None] * norm_gains[1]
        fresh_query = rotate(query_normed, positions[0], positions[1], positions[2]).astype(jnp.bfloat16)
        fresh_key = rotate(key_normed, positions[0], positions[1], positions[2]).astype(jnp.bfloat16)
        own_fresh = jnp.stack([fresh_key, value_rows], axis=1)
        picked = jnp.take_along_axis(
            own_fresh, own_chosen[:, None, :, None], axis=2
        )
        fresh_a = gather_2d(picked[..., :HD], seq_count, z_first=True)
        fresh_b = gather_2d(picked[..., HD:], seq_count, z_first=False)
        full_a = mixed(stale_a, fresh_a, own_fresh[..., :HD], picks_a)
        full_b = mixed(stale_b, fresh_b, own_fresh[..., HD:], picks_b)
        out_a = attend(fresh_query[..., :HD], full_a[:, :, :, 0], full_a[:, :, :, 1], keep_a)
        out_b = attend(fresh_query[..., HD:], full_b[:, :, :, 0], full_b[:, :, :, 1], keep_b)
        attention = jnp.concatenate([out_a, out_b], axis=-1).astype(jnp.bfloat16)
        partial_value = jnp.dot(attention, out_weight, preferred_element_type=jnp.float32)
        pieces = partial_value.reshape(item_count, local_rows, split_count, feature_shard)
        summed = lax.dynamic_index_in_dim(pieces, split_index, 2, keepdims=False)
        for d in range(1, split_count):
            target = (split_index + d) % split_count
            piece = lax.dynamic_index_in_dim(pieces, target, 2, keepdims=False).astype(jnp.bfloat16)
            moved = lax.ppermute(
                piece, "tp", [(i, (i + d) % split_count) for i in range(split_count)]
            )
            summed = summed + moved.astype(jnp.float32)
        result = layer_in.astype(jnp.float32) + gate_shard * summed
        valid_rows = row_slots[None, :] < lengths[:, None]
        return jnp.where(valid_rows[..., None], result, 0.0).astype(jnp.bfloat16)

    first = layer(tokens)
    carried = lax.ppermute(first, "section", [(0, 1)])
    second = layer(carried)
    return jnp.where(section_index == 0, first, second)[None]


def solution(mesh):
    placed = (
        P(None, "seq", "tp"),
        P("section", None, None, "tp"),
        P("section", "tp", None),
        P("section", None, None),
        P("section", None, "tp"),
        P("section", None, None, "seq", "tp"),
        P("section", None, None),
        P(None, None, "seq"),
        P(),
    )
    return jax.shard_map(
        local,
        mesh=mesh,
        in_specs=placed,
        out_specs=P("section", None, "seq", "tp"),
        check_vma=False,
    )
```

```python
import jax
import jax.numpy as jnp
from jax import lax
from jax.sharding import PartitionSpec as P

HD = 128
RECOMP = 4
RING = 8


floor_score = -1e30


def shift_perm(count, step, inner):
    pairs = []
    for s in range(count):
        if inner == 1:
            outer, pos = divmod(s, RING)
            pairs.append((s, ((outer + step) % RING) * RING + pos))
        else:
            outer, pos = divmod(s, RING)
            pairs.append((s, outer * RING + (pos + step) % RING))
    return pairs


def ring_gather(block, count, along_z):
    inner = RING if along_z else 1
    plus = shift_perm(count, 1, inner)
    minus = shift_perm(count, -1, inner)
    rel = [None] * RING
    rel[0] = block
    fwd = block
    bwd = block
    for step in range(1, RING // 2):
        fwd = lax.ppermute(fwd, "seq", plus)
        bwd = lax.ppermute(bwd, "seq", minus)
        rel[RING - step] = fwd
        rel[step] = bwd
    rel[RING // 2] = lax.ppermute(fwd, "seq", plus)
    return jnp.stack(rel)


def gather_2d(block, count, z_first):
    first = ring_gather(block, count, along_z=z_first)
    return ring_gather(first, count, along_z=not z_first)


def rotate(field_rows, frame_place, height_place, width_place):
    lead = field_rows.shape[:-1]
    pair_count = HD // 2
    side_pairs = pair_count // 3
    frame_pairs = pair_count - 2 * side_pairs

    def spacing(pair_total):
        ladder = jnp.arange(pair_total, dtype=jnp.float32)
        return jnp.power(jnp.float32(10000.0), -ladder / pair_total)

    angles = jnp.concatenate(
        [
            frame_place.astype(jnp.float32)[..., None] * spacing(frame_pairs),
            height_place.astype(jnp.float32)[..., None] * spacing(side_pairs),
            width_place.astype(jnp.float32)[..., None] * spacing(side_pairs),
        ],
        axis=-1,
    )
    cosine = jnp.cos(angles)[..., None, :]
    sine_part = jnp.sin(angles)[..., None, :]
    paired = field_rows.reshape(lead + (-1, pair_count, 2))
    first_half = paired[..., 0]
    second = paired[..., 1]
    turned = jnp.stack(
        [first_half * cosine - second * sine_part, first_half * sine_part + second * cosine],
        axis=-1,
    )
    return turned.reshape(lead + (-1,))


def attend(query, keys, values, keep):
    scores = jnp.einsum(
        "iqhd,abikhd->ihqabk", query, keys, preferred_element_type=jnp.float32
    ) * HD ** (-0.5)
    mask = jnp.transpose(keep, (2, 0, 1, 3))[:, None, None]
    scores = jnp.where(mask, scores, floor_score)
    top = jnp.max(scores, axis=(3, 4, 5), keepdims=True)
    weights = jnp.where(mask, jnp.exp(scores - top), 0.0)
    total = jnp.sum(weights, axis=(3, 4, 5))
    numerator = jnp.einsum(
        "ihqabk,abikhd->iqhd", weights.astype(jnp.bfloat16), values, preferred_element_type=jnp.float32
    )
    return numerator / jnp.transpose(total, (0, 2, 1))[..., None]


def local(
    tokens,
    input_weight,
    output_weight,
    modulation,
    norm_gain,
    stale_cache,
    recompute,
    positions,
    lengths,
):
    section_index = lax.axis_index("section")
    seq_count = lax.axis_size("seq")
    patch_index = lax.axis_index("seq")
    split_count = lax.axis_size("tp")
    split_index = lax.axis_index("tp")
    item_count = tokens.shape[0]
    local_rows = tokens.shape[1]
    feature_shard = tokens.shape[2]
    feature_total = feature_shard * split_count
    head_width = input_weight.shape[3]
    head_count = head_width // HD
    joint_weight = input_weight[0].reshape(feature_total, 3 * head_width)
    out_columns = lax.all_to_all(
        output_weight[0].reshape(head_width, split_count, feature_shard), "tp", 1, 0, tiled=True
    ).reshape(head_width * split_count, feature_shard)
    modulate_rows = modulation[0]
    norm_gains = norm_gain[0]
    gate_shard = lax.dynamic_slice_in_dim(
        modulate_rows[2], split_index * feature_shard, feature_shard
    )
    row_y = patch_index // RING
    row_z = patch_index % RING
    local_number = jnp.arange(local_rows, dtype=jnp.int32)
    row_slots = patch_index * local_rows + local_number

    stale = stale_cache[0]
    stale_full = gather_2d(stale, seq_count, z_first=True)

    ring_offsets = jnp.arange(RING, dtype=jnp.int32)
    patch_of = ((row_y + ring_offsets[:, None]) % RING) * RING + (row_z + ring_offsets[None, :]) % RING
    patch_list = patch_of.reshape(-1)
    chosen_all = recompute[0].reshape(item_count, seq_count, RECOMP)
    own_block = (ring_offsets[:, None] == 0) & (ring_offsets[None, :] == 0)
    picks = jnp.take(chosen_all, patch_list, axis=1).reshape(item_count, RING, RING, RECOMP)
    picks = jnp.transpose(picks, (1, 2, 0, 3))
    slots = patch_of[:, :, None, None] * local_rows + local_number
    keep = slots < lengths[None, None, :, None]
    own_chosen = lax.dynamic_slice_in_dim(chosen_all, patch_index, 1, axis=1)[:, 0]

    def mixed(fresh_full, own_fresh):
        out = stale_full
        for r in range(RECOMP):
            hit = local_number[None, None, None, None, :] == picks[:, :, :, None, r : r + 1]
            out = jnp.where(hit[..., None], fresh_full[:, :, :, :, r : r + 1, :], out)
        out = jnp.where(own_block[:, :, None, None, None, None], own_fresh[None, None], out)
        return out

    def layer(layer_in):
        gathered = lax.all_gather(layer_in, "tp", axis=2, tiled=True)
        as_float = gathered.astype(jnp.float32)
        row_mean = jnp.mean(as_float, axis=-1, keepdims=True)
        centered = as_float - row_mean
        variance = jnp.mean(centered * centered, axis=-1, keepdims=True)
        modulated = (
            centered * lax.rsqrt(variance + 1e-06) * (1.0 + modulate_rows[1]) + modulate_rows[0]
        ).astype(jnp.bfloat16)
        projected = jnp.dot(modulated, joint_weight, preferred_element_type=jnp.float32).reshape(
            item_count, local_rows, 3, head_width
        )
        query_raw = projected[:, :, 0]
        key_raw = projected[:, :, 1]
        value_rows = projected[:, :, 2].astype(jnp.bfloat16)
        square_total = lax.psum(
            jnp.stack([jnp.sum(query_raw * query_raw, axis=-1), jnp.sum(key_raw * key_raw, axis=-1)]),
            "tp",
        )
        entry_total = head_width * split_count
        query_normed = (
            query_raw * lax.rsqrt(square_total[0] / entry_total + 1e-06)[..., None] * norm_gains[0]
        )
        key_normed = key_raw * lax.rsqrt(square_total[1] / entry_total + 1e-06)[..., None] * norm_gains[1]
        fresh_query = rotate(query_normed, positions[0], positions[1], positions[2]).astype(jnp.bfloat16)
        fresh_key = rotate(key_normed, positions[0], positions[1], positions[2]).astype(jnp.bfloat16)
        own_fresh = jnp.stack([fresh_key, value_rows], axis=1)
        picked = jnp.take_along_axis(
            own_fresh, own_chosen[:, None, :, None], axis=2
        )
        fresh_all = lax.all_gather(picked, "seq", axis=0, tiled=False)
        fresh_full = jnp.take(fresh_all, patch_list, axis=0).reshape(
            (RING, RING) + fresh_all.shape[1:]
        )
        full = mixed(fresh_full, own_fresh)
        split_heads = full.shape[:4] + (local_rows, head_count, HD)
        full = full.reshape(split_heads)
        attention = attend(
            fresh_query.reshape(item_count, local_rows, head_count, HD),
            full[:, :, :, 0],
            full[:, :, :, 1],
            keep,
        ).reshape(item_count, local_rows, head_width).astype(jnp.bfloat16)
        all_heads = lax.all_gather(attention, "tp", axis=2, tiled=True)
        summed = jnp.dot(all_heads, out_columns, preferred_element_type=jnp.float32)
        result = layer_in.astype(jnp.float32) + gate_shard * summed
        valid_rows = row_slots[None, :] < lengths[:, None]
        return jnp.where(valid_rows[..., None], result, 0.0).astype(jnp.bfloat16)

    first = layer(tokens)
    carried = lax.ppermute(first, "section", [(0, 1)])
    second = layer(carried)
    return jnp.where(section_index == 0, first, second)[None]


def solution(mesh):
    placed = (
        P(None, "seq", "tp"),
        P("section", None, None, "tp"),
        P("section", "tp", None),
        P("section", None, None),
        P("section", None, "tp"),
        P("section", None, None, "seq", "tp"),
        P("section", None, None),
        P(None, None, "seq"),
        P(),
    )
    return jax.shard_map(
        local,
        mesh=mesh,
        in_specs=placed,
        out_specs=P("section", None, "seq", "tp"),
        check_vma=False,
    )
```

```python
import jax
import jax.numpy as jnp
from jax import lax
from jax.sharding import Mesh, PartitionSpec as P

HD = 128
RECOMP = 4


floor_score = -1e30


def ring_gather(block, axis):
    n = lax.axis_size(axis)
    plus = [(i, (i + 1) % n) for i in range(n)]
    minus = [(i, (i - 1) % n) for i in range(n)]
    rel = [None] * n
    rel[0] = block
    fwd = block
    bwd = block
    for step in range(1, n // 2):
        fwd = lax.ppermute(fwd, axis, plus)
        bwd = lax.ppermute(bwd, axis, minus)
        rel[n - step] = fwd
        rel[step] = bwd
    rel[n // 2] = lax.ppermute(fwd, axis, plus)
    return jnp.stack(rel)


def rotate(field_rows, frame_place, height_place, width_place):
    lead = field_rows.shape[:-1]
    pair_count = HD // 2
    side_pairs = pair_count // 3
    frame_pairs = pair_count - 2 * side_pairs

    def spacing(pair_total):
        ladder = jnp.arange(pair_total, dtype=jnp.float32)
        return jnp.power(jnp.float32(10000.0), -ladder / pair_total)

    angles = jnp.concatenate(
        [
            frame_place.astype(jnp.float32)[..., None] * spacing(frame_pairs),
            height_place.astype(jnp.float32)[..., None] * spacing(side_pairs),
            width_place.astype(jnp.float32)[..., None] * spacing(side_pairs),
        ],
        axis=-1,
    )
    cosine = jnp.cos(angles)[..., None, :]
    sine_part = jnp.sin(angles)[..., None, :]
    paired = field_rows.reshape(lead + (-1, pair_count, 2))
    first_half = paired[..., 0]
    second = paired[..., 1]
    turned = jnp.stack(
        [first_half * cosine - second * sine_part, first_half * sine_part + second * cosine],
        axis=-1,
    )
    return turned.reshape(lead + (-1,))


def attend(query, keys, values, keep):
    scores = jnp.einsum(
        "iqhd,abikhd->ihqabk", query, keys, preferred_element_type=jnp.float32
    ) * HD ** (-0.5)
    mask = jnp.transpose(keep, (2, 0, 1, 3))[:, None, None]
    scores = jnp.where(mask, scores, floor_score)
    top = jnp.max(scores, axis=(3, 4, 5), keepdims=True)
    weights = jnp.where(mask, jnp.exp(scores - top), 0.0)
    total = jnp.sum(weights, axis=(3, 4, 5))
    numerator = jnp.einsum(
        "ihqabk,abikhd->iqhd", weights.astype(jnp.bfloat16), values, preferred_element_type=jnp.float32
    )
    return numerator / jnp.transpose(total, (0, 2, 1))[..., None]


def local(
    tokens,
    input_weight,
    output_weight,
    modulation,
    norm_gain,
    stale_cache,
    recompute,
    positions,
    lengths,
):
    section_index = lax.axis_index("section")
    ring = lax.axis_size("sz")
    rows_y = lax.axis_size("sy")
    seq_count = rows_y * ring
    row_y = lax.axis_index("sy")
    row_z = lax.axis_index("sz")
    patch_index = row_y * ring + row_z
    split_count = lax.axis_size("tp")
    split_index = lax.axis_index("tp")
    item_count = tokens.shape[0]
    local_rows = tokens.shape[1]
    feature_shard = tokens.shape[2]
    feature_total = feature_shard * split_count
    head_width = input_weight.shape[3]
    head_count = head_width // HD
    joint_weight = input_weight[0].reshape(feature_total, 3 * head_width)
    out_columns = lax.all_to_all(
        output_weight[0].reshape(head_width, split_count, feature_shard), "tp", 1, 0, tiled=True
    ).reshape(head_width * split_count, feature_shard)
    modulate_rows = modulation[0]
    norm_gains = norm_gain[0]
    gate_shard = lax.dynamic_slice_in_dim(
        modulate_rows[2], split_index * feature_shard, feature_shard
    )
    local_number = jnp.arange(local_rows, dtype=jnp.int32)
    row_slots = patch_index * local_rows + local_number

    stale = stale_cache[0]
    along_z = ring_gather(stale, "sz")
    along_z, tokens = lax.optimization_barrier((along_z, tokens))
    stale_full = ring_gather(along_z, "sy")

    y_offsets = jnp.arange(rows_y, dtype=jnp.int32)
    ring_offsets = jnp.arange(ring, dtype=jnp.int32)
    patch_of = ((row_y + y_offsets[:, None]) % rows_y) * ring + (row_z + ring_offsets[None, :]) % ring
    patch_list = patch_of.reshape(-1)
    chosen_all = recompute[0].reshape(item_count, seq_count, RECOMP)
    own_block = (y_offsets[:, None] == 0) & (ring_offsets[None, :] == 0)
    picks = jnp.take(chosen_all, patch_list, axis=1).reshape(item_count, rows_y, ring, RECOMP)
    picks = jnp.transpose(picks, (1, 2, 0, 3))
    slots = patch_of[:, :, None, None] * local_rows + local_number
    keep = slots < lengths[None, None, :, None]
    own_chosen = lax.dynamic_slice_in_dim(chosen_all, patch_index, 1, axis=1)[:, 0]

    def mixed(fresh_full, own_fresh):
        out = stale_full
        for r in range(RECOMP):
            hit = local_number[None, None, None, None, :] == picks[:, :, :, None, r : r + 1]
            out = jnp.where(hit[..., None], fresh_full[:, :, :, :, r : r + 1, :], out)
        out = jnp.where(own_block[:, :, None, None, None, None], own_fresh[None, None], out)
        return out

    def layer(layer_in):
        gathered = lax.all_gather(layer_in, "tp", axis=2, tiled=True)
        as_float = gathered.astype(jnp.float32)
        row_mean = jnp.mean(as_float, axis=-1, keepdims=True)
        centered = as_float - row_mean
        variance = jnp.mean(centered * centered, axis=-1, keepdims=True)
        modulated = (
            centered * lax.rsqrt(variance + 1e-06) * (1.0 + modulate_rows[1]) + modulate_rows[0]
        ).astype(jnp.bfloat16)
        projected = jnp.dot(modulated, joint_weight, preferred_element_type=jnp.float32).reshape(
            item_count, local_rows, 3, head_width
        )
        query_raw = projected[:, :, 0]
        key_raw = projected[:, :, 1]
        value_rows = projected[:, :, 2].astype(jnp.bfloat16)
        square_total = lax.psum(
            jnp.stack([jnp.sum(query_raw * query_raw, axis=-1), jnp.sum(key_raw * key_raw, axis=-1)]),
            "tp",
        )
        entry_total = head_width * split_count
        query_normed = (
            query_raw * lax.rsqrt(square_total[0] / entry_total + 1e-06)[..., None] * norm_gains[0]
        )
        key_normed = key_raw * lax.rsqrt(square_total[1] / entry_total + 1e-06)[..., None] * norm_gains[1]
        fresh_query = rotate(query_normed, positions[0], positions[1], positions[2]).astype(jnp.bfloat16)
        fresh_key = rotate(key_normed, positions[0], positions[1], positions[2]).astype(jnp.bfloat16)
        own_fresh = jnp.stack([fresh_key, value_rows], axis=1)
        picked = jnp.take_along_axis(
            own_fresh, own_chosen[:, None, :, None], axis=2
        )
        fresh_all = lax.all_gather(lax.all_gather(picked, "sz"), "sy")
        fresh_all = fresh_all.reshape((seq_count,) + picked.shape)
        fresh_full = jnp.take(fresh_all, patch_list, axis=0).reshape((rows_y, ring) + picked.shape)
        full = mixed(fresh_full, own_fresh)
        split_heads = full.shape[:4] + (local_rows, head_count, HD)
        full = full.reshape(split_heads)
        attention = attend(
            fresh_query.reshape(item_count, local_rows, head_count, HD),
            full[:, :, :, 0],
            full[:, :, :, 1],
            keep,
        ).reshape(item_count, local_rows, head_width).astype(jnp.bfloat16)
        all_heads = lax.all_gather(attention, "tp", axis=2, tiled=True)
        summed = jnp.dot(all_heads, out_columns, preferred_element_type=jnp.float32)
        result = layer_in.astype(jnp.float32) + gate_shard * summed
        valid_rows = row_slots[None, :] < lengths[:, None]
        return jnp.where(valid_rows[..., None], result, 0.0).astype(jnp.bfloat16)

    first = layer(tokens)
    carried = lax.ppermute(first, "section", [(0, 1)])
    second = layer(carried)
    return jnp.where(section_index == 0, first, second)[None]


def solution(mesh):
    sizes = dict(mesh.shape)
    inner = 8
    devices = mesh.devices.reshape(sizes["section"], sizes["seq"] // inner, inner, sizes["tp"])
    mesh = Mesh(devices, ("section", "sy", "sz", "tp"))
    seq = ("sy", "sz")
    placed = (
        P(None, seq, "tp"),
        P("section", None, None, "tp"),
        P("section", "tp", None),
        P("section", None, None),
        P("section", None, "tp"),
        P("section", None, None, seq, "tp"),
        P("section", None, None),
        P(None, None, seq),
        P(),
    )
    return jax.shard_map(
        local,
        mesh=mesh,
        in_specs=placed,
        out_specs=P("section", None, seq, "tp"),
        check_vma=False,
    )
```

```python
import jax
import jax.numpy as jnp
from jax import lax
from jax.sharding import Mesh, PartitionSpec as P

HD = 128
RECOMP = 4


floor_score = -1e30


def ring_gather(block, axis):
    n = lax.axis_size(axis)
    plus = [(i, (i + 1) % n) for i in range(n)]
    minus = [(i, (i - 1) % n) for i in range(n)]
    rel = [None] * n
    rel[0] = block
    fwd = block
    bwd = block
    for step in range(1, n // 2):
        fwd = lax.ppermute(fwd, axis, plus)
        bwd = lax.ppermute(bwd, axis, minus)
        rel[n - step] = fwd
        rel[step] = bwd
    rel[n // 2] = lax.ppermute(fwd, axis, plus)
    return jnp.stack(rel)


def spread(x, axis, count):
    send = jnp.broadcast_to(x[None], (count,) + x.shape)
    return lax.all_to_all(send, axis, 0, 0)


def rotate(field_rows, frame_place, height_place, width_place):
    lead = field_rows.shape[:-1]
    pair_count = HD // 2
    side_pairs = pair_count // 3
    frame_pairs = pair_count - 2 * side_pairs

    def spacing(pair_total):
        ladder = jnp.arange(pair_total, dtype=jnp.float32)
        return jnp.power(jnp.float32(10000.0), -ladder / pair_total)

    angles = jnp.concatenate(
        [
            frame_place.astype(jnp.float32)[..., None] * spacing(frame_pairs),
            height_place.astype(jnp.float32)[..., None] * spacing(side_pairs),
            width_place.astype(jnp.float32)[..., None] * spacing(side_pairs),
        ],
        axis=-1,
    )
    cosine = jnp.cos(angles)[..., None, :]
    sine_part = jnp.sin(angles)[..., None, :]
    paired = field_rows.reshape(lead + (-1, pair_count, 2))
    first_half = paired[..., 0]
    second = paired[..., 1]
    turned = jnp.stack(
        [first_half * cosine - second * sine_part, first_half * sine_part + second * cosine],
        axis=-1,
    )
    return turned.reshape(lead + (-1,))


def attend(query, keys, values, keep):
    scores = jnp.einsum(
        "iqhd,abikhd->ihqabk", query, keys, preferred_element_type=jnp.float32
    ) * HD ** (-0.5)
    mask = jnp.transpose(keep, (2, 0, 1, 3))[:, None, None]
    scores = jnp.where(mask, scores, floor_score)
    top = jnp.max(scores, axis=(3, 4, 5), keepdims=True)
    weights = jnp.where(mask, jnp.exp(scores - top), 0.0)
    total = jnp.sum(weights, axis=(3, 4, 5))
    numerator = jnp.einsum(
        "ihqabk,abikhd->iqhd", weights.astype(jnp.bfloat16), values, preferred_element_type=jnp.float32
    )
    return numerator / jnp.transpose(total, (0, 2, 1))[..., None]


def local(
    tokens,
    input_weight,
    output_weight,
    modulation,
    norm_gain,
    stale_cache,
    recompute,
    positions,
    lengths,
):
    section_index = lax.axis_index("section")
    ring = lax.axis_size("sz")
    rows_y = lax.axis_size("sy")
    seq_count = rows_y * ring
    row_y = lax.axis_index("sy")
    row_z = lax.axis_index("sz")
    patch_index = row_y * ring + row_z
    split_count = lax.axis_size("tp")
    split_index = lax.axis_index("tp")
    item_count = tokens.shape[0]
    local_rows = tokens.shape[1]
    feature_shard = tokens.shape[2]
    feature_total = feature_shard * split_count
    head_width = input_weight.shape[3]
    head_count = head_width // HD
    joint_weight = input_weight[0].reshape(feature_total, 3 * head_width)
    out_columns = lax.all_to_all(
        output_weight[0].reshape(head_width, split_count, feature_shard), "tp", 1, 0, tiled=True
    ).reshape(head_width * split_count, feature_shard)
    modulate_rows = modulation[0]
    norm_gains = norm_gain[0]
    gate_shard = lax.dynamic_slice_in_dim(
        modulate_rows[2], split_index * feature_shard, feature_shard
    )
    local_number = jnp.arange(local_rows, dtype=jnp.int32)
    row_slots = patch_index * local_rows + local_number

    stale = stale_cache[0]
    along_z = ring_gather(stale, "sz")
    along_z, tokens = lax.optimization_barrier((along_z, tokens))
    stale_full = ring_gather(along_z, "sy")

    y_offsets = jnp.arange(rows_y, dtype=jnp.int32)
    ring_offsets = jnp.arange(ring, dtype=jnp.int32)
    patch_of = ((row_y + y_offsets[:, None]) % rows_y) * ring + (row_z + ring_offsets[None, :]) % ring
    patch_list = patch_of.reshape(-1)
    chosen_all = recompute[0].reshape(item_count, seq_count, RECOMP)
    own_block = (y_offsets[:, None] == 0) & (ring_offsets[None, :] == 0)
    picks = jnp.take(chosen_all, patch_list, axis=1).reshape(item_count, rows_y, ring, RECOMP)
    picks = jnp.transpose(picks, (1, 2, 0, 3))
    slots = patch_of[:, :, None, None] * local_rows + local_number
    keep = slots < lengths[None, None, :, None]
    own_chosen = lax.dynamic_slice_in_dim(chosen_all, patch_index, 1, axis=1)[:, 0]

    def mixed(fresh_full, own_fresh):
        out = stale_full
        for r in range(RECOMP):
            hit = local_number[None, None, None, None, :] == picks[:, :, :, None, r : r + 1]
            out = jnp.where(hit[..., None], fresh_full[:, :, :, :, r : r + 1, :], out)
        out = jnp.where(own_block[:, :, None, None, None, None], own_fresh[None, None], out)
        return out

    def layer(layer_in):
        gathered = jnp.transpose(spread(layer_in, "tp", split_count), (1, 2, 0, 3)).reshape(
            item_count, local_rows, feature_total
        )
        as_float = gathered.astype(jnp.float32)
        row_mean = jnp.mean(as_float, axis=-1, keepdims=True)
        centered = as_float - row_mean
        variance = jnp.mean(centered * centered, axis=-1, keepdims=True)
        modulated = (
            centered * lax.rsqrt(variance + 1e-06) * (1.0 + modulate_rows[1]) + modulate_rows[0]
        ).astype(jnp.bfloat16)
        projected = jnp.dot(modulated, joint_weight, preferred_element_type=jnp.float32).reshape(
            item_count, local_rows, 3, head_width
        )
        query_raw = projected[:, :, 0]
        key_raw = projected[:, :, 1]
        value_rows = projected[:, :, 2].astype(jnp.bfloat16)
        square_total = jnp.sum(
            spread(
                jnp.stack(
                    [jnp.sum(query_raw * query_raw, axis=-1), jnp.sum(key_raw * key_raw, axis=-1)]
                ),
                "tp",
                split_count,
            ),
            axis=0,
        )
        entry_total = head_width * split_count
        query_normed = (
            query_raw * lax.rsqrt(square_total[0] / entry_total + 1e-06)[..., None] * norm_gains[0]
        )
        key_normed = key_raw * lax.rsqrt(square_total[1] / entry_total + 1e-06)[..., None] * norm_gains[1]
        fresh_query = rotate(query_normed, positions[0], positions[1], positions[2]).astype(jnp.bfloat16)
        fresh_key = rotate(key_normed, positions[0], positions[1], positions[2]).astype(jnp.bfloat16)
        own_fresh = jnp.stack([fresh_key, value_rows], axis=1)
        picked = jnp.take_along_axis(
            own_fresh, own_chosen[:, None, :, None], axis=2
        )
        fresh_all = spread(picked, ("sy", "sz"), seq_count)
        fresh_full = jnp.take(fresh_all, patch_list, axis=0).reshape((rows_y, ring) + picked.shape)
        full = mixed(fresh_full, own_fresh)
        split_heads = full.shape[:4] + (local_rows, head_count, HD)
        full = full.reshape(split_heads)
        attention = attend(
            fresh_query.reshape(item_count, local_rows, head_count, HD),
            full[:, :, :, 0],
            full[:, :, :, 1],
            keep,
        ).reshape(item_count, local_rows, head_width).astype(jnp.bfloat16)
        all_heads = jnp.transpose(spread(attention, "tp", split_count), (1, 2, 0, 3)).reshape(
            item_count, local_rows, head_width * split_count
        )
        summed = jnp.dot(all_heads, out_columns, preferred_element_type=jnp.float32)
        result = layer_in.astype(jnp.float32) + gate_shard * summed
        valid_rows = row_slots[None, :] < lengths[:, None]
        return jnp.where(valid_rows[..., None], result, 0.0).astype(jnp.bfloat16)

    first = layer(tokens)
    carried = lax.ppermute(first, "section", [(0, 1)])
    second = layer(carried)
    return jnp.where(section_index == 0, first, second)[None]


def solution(mesh):
    sizes = dict(mesh.shape)
    inner = 8
    devices = mesh.devices.reshape(sizes["section"], sizes["seq"] // inner, inner, sizes["tp"])
    mesh = Mesh(devices, ("section", "sy", "sz", "tp"))
    seq = ("sy", "sz")
    placed = (
        P(None, seq, "tp"),
        P("section", None, None, "tp"),
        P("section", "tp", None),
        P("section", None, None),
        P("section", None, "tp"),
        P("section", None, None, seq, "tp"),
        P("section", None, None),
        P(None, None, seq),
        P(),
    )
    return jax.shard_map(
        local,
        mesh=mesh,
        in_specs=placed,
        out_specs=P("section", None, seq, "tp"),
        check_vma=False,
    )
```

```python
import jax
import jax.numpy as jnp
from jax import lax
from jax.sharding import Mesh, PartitionSpec as P

HD = 128
RECOMP = 4


floor_score = -1e30


def ring_gather(block, axis):
    n = lax.axis_size(axis)
    plus = [(i, (i + 1) % n) for i in range(n)]
    minus = [(i, (i - 1) % n) for i in range(n)]
    rel = [None] * n
    rel[0] = block
    fwd = block
    bwd = block
    for step in range(1, n // 2):
        fwd = lax.ppermute(fwd, axis, plus)
        bwd = lax.ppermute(bwd, axis, minus)
        rel[n - step] = fwd
        rel[step] = bwd
    rel[n // 2] = lax.ppermute(fwd, axis, plus)
    return jnp.stack(rel)


def spread(x, axis, count):
    send = jnp.broadcast_to(x[None], (count,) + x.shape)
    return lax.all_to_all(send, axis, 0, 0)


def rotate(field_rows, frame_place, height_place, width_place):
    lead = field_rows.shape[:-1]
    pair_count = HD // 2
    side_pairs = pair_count // 3
    frame_pairs = pair_count - 2 * side_pairs

    def spacing(pair_total):
        ladder = jnp.arange(pair_total, dtype=jnp.float32)
        return jnp.power(jnp.float32(10000.0), -ladder / pair_total)

    angles = jnp.concatenate(
        [
            frame_place.astype(jnp.float32)[..., None] * spacing(frame_pairs),
            height_place.astype(jnp.float32)[..., None] * spacing(side_pairs),
            width_place.astype(jnp.float32)[..., None] * spacing(side_pairs),
        ],
        axis=-1,
    )
    cosine = jnp.cos(angles)[..., None, :]
    sine_part = jnp.sin(angles)[..., None, :]
    paired = field_rows.reshape(lead + (-1, pair_count, 2))
    first_half = paired[..., 0]
    second = paired[..., 1]
    turned = jnp.stack(
        [first_half * cosine - second * sine_part, first_half * sine_part + second * cosine],
        axis=-1,
    )
    return turned.reshape(lead + (-1,))


def attend(query, groups):
    scored = []
    for keys, values, keep, score_spec, value_spec in groups:
        scores = jnp.einsum(score_spec, query, keys, preferred_element_type=jnp.float32) * HD ** (-0.5)
        scores = jnp.where(keep, scores, floor_score)
        scored.append(scores)
    key_axes = [tuple(range(2, x.ndim)) for x in scored]
    top = scored[0].max(axis=key_axes[0])
    for scores, axes in zip(scored[1:], key_axes[1:]):
        top = jnp.maximum(top, scores.max(axis=axes))
    total = 0.0
    numerator = 0.0
    for scores, axes, (keys, values, keep, score_spec, value_spec) in zip(scored, key_axes, groups):
        top_b = top.reshape(top.shape + (1,) * len(axes))
        weights = jnp.where(keep, jnp.exp(scores - top_b), 0.0)
        total = total + jnp.sum(weights, axis=axes)
        numerator = numerator + jnp.einsum(
            value_spec, weights.astype(jnp.bfloat16), values, preferred_element_type=jnp.float32
        )
    return numerator / total[..., None]


def heads_first(x):
    lead = x.shape[:-1]
    return jnp.transpose(x.reshape(lead + (-1, HD)), (3, 1, 0, 2, 4))


def local(
    tokens,
    input_weight,
    output_weight,
    modulation,
    norm_gain,
    stale_cache,
    recompute,
    positions,
    lengths,
):
    section_index = lax.axis_index("section")
    ring = lax.axis_size("sz")
    rows_y = lax.axis_size("sy")
    seq_count = rows_y * ring
    row_y = lax.axis_index("sy")
    row_z = lax.axis_index("sz")
    patch_index = row_y * ring + row_z
    split_count = lax.axis_size("tp")
    split_index = lax.axis_index("tp")
    item_count = tokens.shape[0]
    local_rows = tokens.shape[1]
    feature_shard = tokens.shape[2]
    feature_total = feature_shard * split_count
    head_width = input_weight.shape[3]
    head_count = head_width // HD
    joint_weight = input_weight[0].reshape(feature_total, 3 * head_width)
    out_columns = lax.all_to_all(
        output_weight[0].reshape(head_width, split_count, feature_shard), "tp", 1, 0, tiled=True
    ).reshape(head_width * split_count, feature_shard)
    modulate_rows = modulation[0]
    norm_gains = norm_gain[0]
    gate_shard = lax.dynamic_slice_in_dim(
        modulate_rows[2], split_index * feature_shard, feature_shard
    )
    local_number = jnp.arange(local_rows, dtype=jnp.int32)
    row_slots = patch_index * local_rows + local_number

    stale = heads_first(stale_cache[0])
    first_a = ring_gather(stale[0], "sz")
    first_b = ring_gather(stale[1], "sy")
    first_a, first_b, tokens = lax.optimization_barrier((first_a, first_b, tokens))
    stale_a = ring_gather(first_a, "sy")
    stale_b = ring_gather(first_b, "sz")

    y_offsets = jnp.arange(rows_y, dtype=jnp.int32)
    ring_offsets = jnp.arange(ring, dtype=jnp.int32)
    patch_a = ((row_y + y_offsets[:, None]) % rows_y) * ring + (row_z + ring_offsets[None, :]) % ring
    patch_b = ((row_y + y_offsets[None, :]) % rows_y) * ring + (row_z + ring_offsets[:, None]) % ring
    chosen_all = recompute[0].reshape(item_count, seq_count, RECOMP)
    own_chosen = lax.dynamic_slice_in_dim(chosen_all, patch_index, 1, axis=1)[:, 0]

    def stale_keep(patch_of):
        picks = jnp.take(chosen_all, patch_of.reshape(-1), axis=1).reshape(
            (item_count,) + patch_of.shape + (RECOMP,)
        )
        recomputed = jnp.any(local_number[:, None] == picks[..., None, :], axis=-1)
        slots = patch_of[..., None] * local_rows + local_number
        live = slots[None] < lengths[:, None, None, None]
        other = (patch_of != patch_index)[None, :, :, None]
        return (live & other & ~recomputed)[:, None]

    keep_a = stale_keep(patch_a)
    keep_b = stale_keep(patch_b)
    all_patches = jnp.arange(seq_count, dtype=jnp.int32)
    fresh_slots = all_patches[None, :, None] * local_rows + chosen_all
    keep_fresh = (
        (fresh_slots < lengths[:, None, None]) & (all_patches != patch_index)[None, :, None]
    )[:, None]
    keep_own = (row_slots[None, :] < lengths[:, None])[:, None]

    def layer(layer_in):
        gathered = jnp.transpose(spread(layer_in, "tp", split_count), (1, 2, 0, 3)).reshape(
            item_count, local_rows, feature_total
        )
        as_float = gathered.astype(jnp.float32)
        row_mean = jnp.mean(as_float, axis=-1, keepdims=True)
        centered = as_float - row_mean
        variance = jnp.mean(centered * centered, axis=-1, keepdims=True)
        modulated = (
            centered * lax.rsqrt(variance + 1e-06) * (1.0 + modulate_rows[1]) + modulate_rows[0]
        ).astype(jnp.bfloat16)
        projected = jnp.dot(modulated, joint_weight, preferred_element_type=jnp.float32).reshape(
            item_count, local_rows, 3, head_width
        )
        query_raw = projected[:, :, 0]
        key_raw = projected[:, :, 1]
        value_rows = projected[:, :, 2].astype(jnp.bfloat16)
        square_total = jnp.sum(
            spread(
                jnp.stack(
                    [jnp.sum(query_raw * query_raw, axis=-1), jnp.sum(key_raw * key_raw, axis=-1)]
                ),
                "tp",
                split_count,
            ),
            axis=0,
        )
        entry_total = head_width * split_count
        query_normed = (
            query_raw * lax.rsqrt(square_total[0] / entry_total + 1e-06)[..., None] * norm_gains[0]
        )
        key_normed = key_raw * lax.rsqrt(square_total[1] / entry_total + 1e-06)[..., None] * norm_gains[1]
        fresh_query = rotate(query_normed, positions[0], positions[1], positions[2]).astype(jnp.bfloat16)
        fresh_key = rotate(key_normed, positions[0], positions[1], positions[2]).astype(jnp.bfloat16)
        own_fresh = jnp.stack([fresh_key, value_rows], axis=1)
        picked = jnp.take_along_axis(
            own_fresh, own_chosen[:, None, :, None], axis=2
        )
        fresh_all = spread(heads_first(picked), ("sy", "sz"), seq_count)
        outs = []
        for head, stale_h in enumerate((stale_a, stale_b)):
            cols = slice(head * HD, (head + 1) * HD)
            keep_h = (keep_a, keep_b)[head]
            groups = (
                (stale_h[:, :, 0], stale_h[:, :, 1], keep_h, "iqd,abikd->iqabk", "iqabk,abikd->iqd"),
                (
                    fresh_all[:, head, 0],
                    fresh_all[:, head, 1],
                    keep_fresh,
                    "iqd,pird->iqpr",
                    "iqpr,pird->iqd",
                ),
                (fresh_key[..., cols], value_rows[..., cols], keep_own, "iqd,ikd->iqk", "iqk,ikd->iqd"),
            )
            outs.append(attend(fresh_query[..., cols], groups))
        attention = jnp.concatenate(outs, axis=-1).astype(jnp.bfloat16)
        all_heads = jnp.transpose(spread(attention, "tp", split_count), (1, 2, 0, 3)).reshape(
            item_count, local_rows, head_width * split_count
        )
        summed = jnp.dot(all_heads, out_columns, preferred_element_type=jnp.float32)
        result = layer_in.astype(jnp.float32) + gate_shard * summed
        valid_rows = row_slots[None, :] < lengths[:, None]
        return jnp.where(valid_rows[..., None], result, 0.0).astype(jnp.bfloat16)

    first = layer(tokens)
    carried = lax.ppermute(first, "section", [(0, 1)])
    second = layer(carried)
    return jnp.where(section_index == 0, first, second)[None]


def solution(mesh):
    sizes = dict(mesh.shape)
    inner = 8
    devices = mesh.devices.reshape(sizes["section"], sizes["seq"] // inner, inner, sizes["tp"])
    mesh = Mesh(devices, ("section", "sy", "sz", "tp"))
    seq = ("sy", "sz")
    placed = (
        P(None, seq, "tp"),
        P("section", None, None, "tp"),
        P("section", "tp", None),
        P("section", None, None),
        P("section", None, "tp"),
        P("section", None, None, seq, "tp"),
        P("section", None, None),
        P(None, None, seq),
        P(),
    )
    return jax.shard_map(
        local,
        mesh=mesh,
        in_specs=placed,
        out_specs=P("section", None, seq, "tp"),
        check_vma=False,
    )
```

```python
import jax
import jax.numpy as jnp
from jax import lax
from jax.sharding import Mesh, PartitionSpec as P

HD = 128
RECOMP = 4


floor_score = -1e30


def ring_gather(block, axis):
    n = lax.axis_size(axis)
    plus = [(i, (i + 1) % n) for i in range(n)]
    minus = [(i, (i - 1) % n) for i in range(n)]
    rel = [None] * n
    rel[0] = block
    fwd = block
    bwd = block
    for step in range(1, n // 2):
        fwd = lax.ppermute(fwd, axis, plus)
        bwd = lax.ppermute(bwd, axis, minus)
        rel[n - step] = fwd
        rel[step] = bwd
    rel[n // 2] = lax.ppermute(fwd, axis, plus)
    return jnp.stack(rel)


def spread(x, axis, count):
    send = jnp.broadcast_to(x[None], (count,) + x.shape)
    return lax.all_to_all(send, axis, 0, 0)


def rotate(field_rows, frame_place, height_place, width_place):
    lead = field_rows.shape[:-1]
    pair_count = HD // 2
    side_pairs = pair_count // 3
    frame_pairs = pair_count - 2 * side_pairs

    def spacing(pair_total):
        ladder = jnp.arange(pair_total, dtype=jnp.float32)
        return jnp.power(jnp.float32(10000.0), -ladder / pair_total)

    angles = jnp.concatenate(
        [
            frame_place.astype(jnp.float32)[..., None] * spacing(frame_pairs),
            height_place.astype(jnp.float32)[..., None] * spacing(side_pairs),
            width_place.astype(jnp.float32)[..., None] * spacing(side_pairs),
        ],
        axis=-1,
    )
    cosine = jnp.cos(angles)[..., None, :]
    sine_part = jnp.sin(angles)[..., None, :]
    paired = field_rows.reshape(lead + (-1, pair_count, 2))
    first_half = paired[..., 0]
    second = paired[..., 1]
    turned = jnp.stack(
        [first_half * cosine - second * sine_part, first_half * sine_part + second * cosine],
        axis=-1,
    )
    return turned.reshape(lead + (-1,))


def attend(query, groups):
    scored = []
    for keys, values, keep, score_spec, value_spec in groups:
        scores = jnp.einsum(score_spec, query, keys, preferred_element_type=jnp.float32) * HD ** (-0.5)
        scores = jnp.where(keep, scores, floor_score)
        scored.append(scores)
    key_axes = [tuple(range(2, x.ndim)) for x in scored]
    top = scored[0].max(axis=key_axes[0])
    for scores, axes in zip(scored[1:], key_axes[1:]):
        top = jnp.maximum(top, scores.max(axis=axes))
    total = 0.0
    numerator = 0.0
    for scores, axes, (keys, values, keep, score_spec, value_spec) in zip(scored, key_axes, groups):
        top_b = top.reshape(top.shape + (1,) * len(axes))
        weights = jnp.where(keep, jnp.exp(scores - top_b), 0.0)
        total = total + jnp.sum(weights, axis=axes)
        numerator = numerator + jnp.einsum(
            value_spec, weights.astype(jnp.bfloat16), values, preferred_element_type=jnp.float32
        )
    return numerator / total[..., None]


def heads_first(x):
    lead = x.shape[:-1]
    return jnp.transpose(x.reshape(lead + (-1, HD)), (3, 1, 0, 2, 4))


def local(
    tokens,
    input_weight,
    output_weight,
    modulation,
    norm_gain,
    stale_cache,
    recompute,
    positions,
    lengths,
):
    section_index = lax.axis_index("section")
    ring = lax.axis_size("sz")
    rows_y = lax.axis_size("sy")
    seq_count = rows_y * ring
    row_y = lax.axis_index("sy")
    row_z = lax.axis_index("sz")
    patch_index = row_y * ring + row_z
    split_count = lax.axis_size("tp")
    split_index = lax.axis_index("tp")
    item_count = tokens.shape[0]
    local_rows = tokens.shape[1]
    feature_shard = tokens.shape[2]
    feature_total = feature_shard * split_count
    head_width = input_weight.shape[3]
    head_count = head_width // HD
    joint_weight = input_weight[0].reshape(feature_total, 3 * head_width)
    out_full = lax.all_gather(output_weight[0], "tp", axis=0, tiled=True)
    modulate_rows = modulation[0]
    norm_gains = norm_gain[0]
    local_number = jnp.arange(local_rows, dtype=jnp.int32)
    row_slots = patch_index * local_rows + local_number

    stale = heads_first(stale_cache[0])
    first_a = spread(stale[0], "sz", ring)
    first_b = spread(stale[1], "sy", rows_y)
    first_a, first_b, tokens = lax.optimization_barrier((first_a, first_b, tokens))
    stale_a = ring_gather(first_a, "sy")
    stale_b = ring_gather(first_b, "sz")

    y_offsets = jnp.arange(rows_y, dtype=jnp.int32)
    ring_offsets = jnp.arange(ring, dtype=jnp.int32)
    patch_a = ((row_y + y_offsets[:, None]) % rows_y) * ring + ring_offsets[None, :]
    patch_b = y_offsets[None, :] * ring + (row_z + ring_offsets[:, None]) % ring
    chosen_all = recompute[0].reshape(item_count, seq_count, RECOMP)
    own_chosen = lax.dynamic_slice_in_dim(chosen_all, patch_index, 1, axis=1)[:, 0]

    def stale_keep(patch_of):
        picks = jnp.take(chosen_all, patch_of.reshape(-1), axis=1).reshape(
            (item_count,) + patch_of.shape + (RECOMP,)
        )
        recomputed = jnp.any(local_number[:, None] == picks[..., None, :], axis=-1)
        slots = patch_of[..., None] * local_rows + local_number
        live = slots[None] < lengths[:, None, None, None]
        other = (patch_of != patch_index)[None, :, :, None]
        return (live & other & ~recomputed)[:, None]

    keep_a = stale_keep(patch_a)
    keep_b = stale_keep(patch_b)
    all_patches = jnp.arange(seq_count, dtype=jnp.int32)
    fresh_slots = all_patches[None, :, None] * local_rows + chosen_all
    keep_fresh = (
        (fresh_slots < lengths[:, None, None]) & (all_patches != patch_index)[None, :, None]
    )[:, None]
    keep_own = (row_slots[None, :] < lengths[:, None])[:, None]

    def layer(gathered):
        as_float = gathered.astype(jnp.float32)
        row_mean = jnp.mean(as_float, axis=-1, keepdims=True)
        centered = as_float - row_mean
        variance = jnp.mean(centered * centered, axis=-1, keepdims=True)
        modulated = (
            centered * lax.rsqrt(variance + 1e-06) * (1.0 + modulate_rows[1]) + modulate_rows[0]
        ).astype(jnp.bfloat16)
        projected = jnp.dot(modulated, joint_weight, preferred_element_type=jnp.float32).reshape(
            item_count, local_rows, 3, head_width
        )
        query_raw = projected[:, :, 0]
        key_raw = projected[:, :, 1]
        value_rows = projected[:, :, 2].astype(jnp.bfloat16)
        square_total = jnp.sum(
            spread(
                jnp.stack(
                    [jnp.sum(query_raw * query_raw, axis=-1), jnp.sum(key_raw * key_raw, axis=-1)]
                ),
                "tp",
                split_count,
            ),
            axis=0,
        )
        entry_total = head_width * split_count
        query_normed = (
            query_raw * lax.rsqrt(square_total[0] / entry_total + 1e-06)[..., None] * norm_gains[0]
        )
        key_normed = key_raw * lax.rsqrt(square_total[1] / entry_total + 1e-06)[..., None] * norm_gains[1]
        fresh_query = rotate(query_normed, positions[0], positions[1], positions[2]).astype(jnp.bfloat16)
        fresh_key = rotate(key_normed, positions[0], positions[1], positions[2]).astype(jnp.bfloat16)
        own_fresh = jnp.stack([fresh_key, value_rows], axis=1)
        picked = jnp.take_along_axis(
            own_fresh, own_chosen[:, None, :, None], axis=2
        )
        fresh_all = spread(heads_first(picked), ("sy", "sz"), seq_count)
        outs = []
        for head, stale_h in enumerate((stale_a, stale_b)):
            cols = slice(head * HD, (head + 1) * HD)
            keep_h = (keep_a, keep_b)[head]
            groups = (
                (stale_h[:, :, 0], stale_h[:, :, 1], keep_h, "iqd,abikd->iqabk", "iqabk,abikd->iqd"),
                (
                    fresh_all[:, head, 0],
                    fresh_all[:, head, 1],
                    keep_fresh,
                    "iqd,pird->iqpr",
                    "iqpr,pird->iqd",
                ),
                (fresh_key[..., cols], value_rows[..., cols], keep_own, "iqd,ikd->iqk", "iqk,ikd->iqd"),
            )
            outs.append(attend(fresh_query[..., cols], groups))
        attention = jnp.concatenate(outs, axis=-1).astype(jnp.bfloat16)
        all_heads = jnp.transpose(spread(attention, "tp", split_count), (1, 2, 0, 3)).reshape(
            item_count, local_rows, head_width * split_count
        )
        summed = jnp.dot(all_heads, out_full, preferred_element_type=jnp.float32)
        result = as_float + modulate_rows[2] * summed
        valid_rows = row_slots[None, :] < lengths[:, None]
        return jnp.where(valid_rows[..., None], result, 0.0).astype(jnp.bfloat16)

    whole_tokens = jnp.transpose(spread(tokens, "tp", split_count), (1, 2, 0, 3)).reshape(
        item_count, local_rows, feature_total
    )
    first = layer(whole_tokens)
    carried = lax.ppermute(first, "section", [(0, 1)])
    second = layer(carried)
    chosen_rows = jnp.where(section_index == 0, first, second)
    own_part = lax.dynamic_slice_in_dim(chosen_rows, split_index * feature_shard, feature_shard, axis=2)
    return own_part[None]


def solution(mesh):
    sizes = dict(mesh.shape)
    inner = 8
    devices = mesh.devices.reshape(sizes["section"], sizes["seq"] // inner, inner, sizes["tp"])
    mesh = Mesh(devices, ("section", "sy", "sz", "tp"))
    seq = ("sy", "sz")
    placed = (
        P(None, seq, "tp"),
        P("section", None, None, "tp"),
        P("section", "tp", None),
        P("section", None, None),
        P("section", None, "tp"),
        P("section", None, None, seq, "tp"),
        P("section", None, None),
        P(None, None, seq),
        P(),
    )
    return jax.shard_map(
        local,
        mesh=mesh,
        in_specs=placed,
        out_specs=P("section", None, seq, "tp"),
        check_vma=False,
    )
```

```python
import jax
import jax.numpy as jnp
from jax import lax
from jax.sharding import Mesh, PartitionSpec as P

HD = 128
RECOMP = 4


floor_score = -1e30


def ring_gather(block, axis):
    n = lax.axis_size(axis)
    plus = [(i, (i + 1) % n) for i in range(n)]
    minus = [(i, (i - 1) % n) for i in range(n)]
    rel = [None] * n
    rel[0] = block
    fwd = block
    bwd = block
    for step in range(1, n // 2):
        fwd = lax.ppermute(fwd, axis, plus)
        bwd = lax.ppermute(bwd, axis, minus)
        rel[n - step] = fwd
        rel[step] = bwd
    rel[n // 2] = lax.ppermute(fwd, axis, plus)
    return jnp.stack(rel)


def spread(x, axis, count):
    send = jnp.broadcast_to(x[None], (count,) + x.shape)
    return lax.all_to_all(send, axis, 0, 0)


def rotate(field_rows, frame_place, height_place, width_place):
    lead = field_rows.shape[:-1]
    pair_count = HD // 2
    side_pairs = pair_count // 3
    frame_pairs = pair_count - 2 * side_pairs

    def spacing(pair_total):
        ladder = jnp.arange(pair_total, dtype=jnp.float32)
        return jnp.power(jnp.float32(10000.0), -ladder / pair_total)

    angles = jnp.concatenate(
        [
            frame_place.astype(jnp.float32)[..., None] * spacing(frame_pairs),
            height_place.astype(jnp.float32)[..., None] * spacing(side_pairs),
            width_place.astype(jnp.float32)[..., None] * spacing(side_pairs),
        ],
        axis=-1,
    )
    cosine = jnp.cos(angles)[..., None, :]
    sine_part = jnp.sin(angles)[..., None, :]
    paired = field_rows.reshape(lead + (-1, pair_count, 2))
    first_half = paired[..., 0]
    second = paired[..., 1]
    turned = jnp.stack(
        [first_half * cosine - second * sine_part, first_half * sine_part + second * cosine],
        axis=-1,
    )
    return turned.reshape(lead + (-1,))


def attend(query, groups):
    scored = []
    for keys, values, keep, score_spec, value_spec in groups:
        scores = jnp.einsum(score_spec, query, keys, preferred_element_type=jnp.float32) * HD ** (-0.5)
        scores = jnp.where(keep, scores, floor_score)
        scored.append(scores)
    key_axes = [tuple(range(2, x.ndim)) for x in scored]
    top = scored[0].max(axis=key_axes[0])
    for scores, axes in zip(scored[1:], key_axes[1:]):
        top = jnp.maximum(top, scores.max(axis=axes))
    total = 0.0
    numerator = 0.0
    for scores, axes, (keys, values, keep, score_spec, value_spec) in zip(scored, key_axes, groups):
        top_b = top.reshape(top.shape + (1,) * len(axes))
        weights = jnp.where(keep, jnp.exp(scores - top_b), 0.0)
        total = total + jnp.sum(weights, axis=axes)
        numerator = numerator + jnp.einsum(
            value_spec, weights.astype(jnp.bfloat16), values, preferred_element_type=jnp.float32
        )
    return numerator / total[..., None]


def heads_first(x):
    lead = x.shape[:-1]
    return jnp.transpose(x.reshape(lead + (-1, HD)), (3, 1, 0, 2, 4))


def local(
    tokens,
    input_weight,
    output_weight,
    modulation,
    norm_gain,
    stale_cache,
    recompute,
    positions,
    lengths,
):
    section_index = lax.axis_index("section")
    ring = lax.axis_size("sz")
    rows_y = lax.axis_size("sy")
    seq_count = rows_y * ring
    row_y = lax.axis_index("sy")
    row_z = lax.axis_index("sz")
    patch_index = row_y * ring + row_z
    split_count = lax.axis_size("tp")
    split_index = lax.axis_index("tp")
    item_count = tokens.shape[0]
    local_rows = tokens.shape[1]
    feature_shard = tokens.shape[2]
    feature_total = feature_shard * split_count
    head_width = input_weight.shape[3]
    head_count = head_width // HD
    joint_weight = input_weight[0].reshape(feature_total, 3 * head_width)
    norm_weight = lax.all_gather(input_weight[0][:, :2], "tp", axis=2, tiled=True).reshape(
        feature_total, 2 * head_width * split_count
    )
    out_full = lax.all_gather(output_weight[0], "tp", axis=0, tiled=True)
    modulate_rows = modulation[0]
    norm_gains = norm_gain[0]
    local_number = jnp.arange(local_rows, dtype=jnp.int32)
    row_slots = patch_index * local_rows + local_number

    stale = heads_first(stale_cache[0])
    first_a = spread(stale[0], "sz", ring)
    first_b = spread(stale[1], "sy", rows_y)
    first_a, first_b, tokens = lax.optimization_barrier((first_a, first_b, tokens))
    stale_a = ring_gather(first_a, "sy")
    stale_b = ring_gather(first_b, "sz")

    y_offsets = jnp.arange(rows_y, dtype=jnp.int32)
    ring_offsets = jnp.arange(ring, dtype=jnp.int32)
    patch_a = ((row_y + y_offsets[:, None]) % rows_y) * ring + ring_offsets[None, :]
    patch_b = y_offsets[None, :] * ring + (row_z + ring_offsets[:, None]) % ring
    chosen_all = recompute[0].reshape(item_count, seq_count, RECOMP)
    own_chosen = lax.dynamic_slice_in_dim(chosen_all, patch_index, 1, axis=1)[:, 0]

    def stale_keep(patch_of):
        picks = jnp.take(chosen_all, patch_of.reshape(-1), axis=1).reshape(
            (item_count,) + patch_of.shape + (RECOMP,)
        )
        recomputed = jnp.any(local_number[:, None] == picks[..., None, :], axis=-1)
        slots = patch_of[..., None] * local_rows + local_number
        live = slots[None] < lengths[:, None, None, None]
        other = (patch_of != patch_index)[None, :, :, None]
        return (live & other & ~recomputed)[:, None]

    keep_a = stale_keep(patch_a)
    keep_b = stale_keep(patch_b)
    all_patches = jnp.arange(seq_count, dtype=jnp.int32)
    fresh_slots = all_patches[None, :, None] * local_rows + chosen_all
    keep_fresh = (
        (fresh_slots < lengths[:, None, None]) & (all_patches != patch_index)[None, :, None]
    )[:, None]
    keep_own = (row_slots[None, :] < lengths[:, None])[:, None]

    def layer(gathered):
        as_float = gathered.astype(jnp.float32)
        row_mean = jnp.mean(as_float, axis=-1, keepdims=True)
        centered = as_float - row_mean
        variance = jnp.mean(centered * centered, axis=-1, keepdims=True)
        modulated = (
            centered * lax.rsqrt(variance + 1e-06) * (1.0 + modulate_rows[1]) + modulate_rows[0]
        ).astype(jnp.bfloat16)
        projected = jnp.dot(modulated, joint_weight, preferred_element_type=jnp.float32).reshape(
            item_count, local_rows, 3, head_width
        )
        query_raw = projected[:, :, 0]
        key_raw = projected[:, :, 1]
        value_rows = projected[:, :, 2].astype(jnp.bfloat16)
        every_head = jnp.dot(modulated, norm_weight, preferred_element_type=jnp.float32).reshape(
            item_count, local_rows, 2, head_width * split_count
        )
        square_total = jnp.moveaxis(jnp.sum(every_head * every_head, axis=-1), -1, 0)
        entry_total = head_width * split_count
        query_normed = (
            query_raw * lax.rsqrt(square_total[0] / entry_total + 1e-06)[..., None] * norm_gains[0]
        )
        key_normed = key_raw * lax.rsqrt(square_total[1] / entry_total + 1e-06)[..., None] * norm_gains[1]
        fresh_query = rotate(query_normed, positions[0], positions[1], positions[2]).astype(jnp.bfloat16)
        fresh_key = rotate(key_normed, positions[0], positions[1], positions[2]).astype(jnp.bfloat16)
        own_fresh = jnp.stack([fresh_key, value_rows], axis=1)
        picked = jnp.take_along_axis(
            own_fresh, own_chosen[:, None, :, None], axis=2
        )
        fresh_all = spread(heads_first(picked), ("sy", "sz"), seq_count)
        outs = []
        for head, stale_h in enumerate((stale_a, stale_b)):
            cols = slice(head * HD, (head + 1) * HD)
            keep_h = (keep_a, keep_b)[head]
            groups = (
                (stale_h[:, :, 0], stale_h[:, :, 1], keep_h, "iqd,abikd->iqabk", "iqabk,abikd->iqd"),
                (
                    fresh_all[:, head, 0],
                    fresh_all[:, head, 1],
                    keep_fresh,
                    "iqd,pird->iqpr",
                    "iqpr,pird->iqd",
                ),
                (fresh_key[..., cols], value_rows[..., cols], keep_own, "iqd,ikd->iqk", "iqk,ikd->iqd"),
            )
            outs.append(attend(fresh_query[..., cols], groups))
        attention = jnp.concatenate(outs, axis=-1).astype(jnp.bfloat16)
        all_heads = jnp.transpose(spread(attention, "tp", split_count), (1, 2, 0, 3)).reshape(
            item_count, local_rows, head_width * split_count
        )
        summed = jnp.dot(all_heads, out_full, preferred_element_type=jnp.float32)
        result = as_float + modulate_rows[2] * summed
        valid_rows = row_slots[None, :] < lengths[:, None]
        return jnp.where(valid_rows[..., None], result, 0.0).astype(jnp.bfloat16)

    whole_tokens = jnp.transpose(spread(tokens, "tp", split_count), (1, 2, 0, 3)).reshape(
        item_count, local_rows, feature_total
    )
    first = layer(whole_tokens)
    carried = lax.ppermute(first, "section", [(0, 1)])
    second = layer(carried)
    chosen_rows = jnp.where(section_index == 0, first, second)
    own_part = lax.dynamic_slice_in_dim(chosen_rows, split_index * feature_shard, feature_shard, axis=2)
    return own_part[None]


def solution(mesh):
    sizes = dict(mesh.shape)
    inner = 8
    devices = mesh.devices.reshape(sizes["section"], sizes["seq"] // inner, inner, sizes["tp"])
    mesh = Mesh(devices, ("section", "sy", "sz", "tp"))
    seq = ("sy", "sz")
    placed = (
        P(None, seq, "tp"),
        P("section", None, None, "tp"),
        P("section", "tp", None),
        P("section", None, None),
        P("section", None, "tp"),
        P("section", None, None, seq, "tp"),
        P("section", None, None),
        P(None, None, seq),
        P(),
    )
    return jax.shard_map(
        local,
        mesh=mesh,
        in_specs=placed,
        out_specs=P("section", None, seq, "tp"),
        check_vma=False,
    )
```

```python
import jax
import jax.numpy as jnp
from jax import lax
from jax.sharding import Mesh, PartitionSpec as P

HD = 128
RECOMP = 4


floor_score = -1e30


def ring_gather(block, axis):
    n = lax.axis_size(axis)
    plus = [(i, (i + 1) % n) for i in range(n)]
    minus = [(i, (i - 1) % n) for i in range(n)]
    rel = [None] * n
    rel[0] = block
    fwd = block
    bwd = block
    for step in range(1, n // 2):
        fwd = lax.ppermute(fwd, axis, plus)
        bwd = lax.ppermute(bwd, axis, minus)
        rel[n - step] = fwd
        rel[step] = bwd
    rel[n // 2] = lax.ppermute(fwd, axis, plus)
    return jnp.stack(rel)


def spread(x, axis, count):
    send = jnp.broadcast_to(x[None], (count,) + x.shape)
    return lax.all_to_all(send, axis, 0, 0)


def rotate(field_rows, frame_place, height_place, width_place):
    lead = field_rows.shape[:-1]
    pair_count = HD // 2
    side_pairs = pair_count // 3
    frame_pairs = pair_count - 2 * side_pairs

    def spacing(pair_total):
        ladder = jnp.arange(pair_total, dtype=jnp.float32)
        return jnp.power(jnp.float32(10000.0), -ladder / pair_total)

    angles = jnp.concatenate(
        [
            frame_place.astype(jnp.float32)[..., None] * spacing(frame_pairs),
            height_place.astype(jnp.float32)[..., None] * spacing(side_pairs),
            width_place.astype(jnp.float32)[..., None] * spacing(side_pairs),
        ],
        axis=-1,
    )
    cosine = jnp.cos(angles)[..., None, :]
    sine_part = jnp.sin(angles)[..., None, :]
    paired = field_rows.reshape(lead + (-1, pair_count, 2))
    first_half = paired[..., 0]
    second = paired[..., 1]
    turned = jnp.stack(
        [first_half * cosine - second * sine_part, first_half * sine_part + second * cosine],
        axis=-1,
    )
    return turned.reshape(lead + (-1,))


def attend(query, groups):
    scored = []
    for keys, values, keep, score_spec, value_spec in groups:
        scores = jnp.einsum(score_spec, query, keys, preferred_element_type=jnp.float32) * HD ** (-0.5)
        scores = jnp.where(keep, scores, floor_score)
        scored.append(scores)
    key_axes = [tuple(range(2, x.ndim)) for x in scored]
    top = scored[0].max(axis=key_axes[0])
    for scores, axes in zip(scored[1:], key_axes[1:]):
        top = jnp.maximum(top, scores.max(axis=axes))
    total = 0.0
    numerator = 0.0
    for scores, axes, (keys, values, keep, score_spec, value_spec) in zip(scored, key_axes, groups):
        top_b = top.reshape(top.shape + (1,) * len(axes))
        weights = jnp.where(keep, jnp.exp(scores - top_b), 0.0)
        total = total + jnp.sum(weights, axis=axes)
        numerator = numerator + jnp.einsum(
            value_spec, weights.astype(jnp.bfloat16), values, preferred_element_type=jnp.float32
        )
    return numerator / total[..., None]


def heads_first(x):
    lead = x.shape[:-1]
    return jnp.transpose(x.reshape(lead + (-1, HD)), (3, 1, 0, 2, 4))


def local(
    tokens,
    input_weight,
    output_weight,
    modulation,
    norm_gain,
    stale_cache,
    recompute,
    positions,
    lengths,
):
    section_index = lax.axis_index("section")
    ring = lax.axis_size("sz")
    rows_y = lax.axis_size("sy")
    seq_count = rows_y * ring
    row_y = lax.axis_index("sy")
    row_z = lax.axis_index("sz")
    patch_index = row_y * ring + row_z
    split_count = lax.axis_size("tp")
    split_index = lax.axis_index("tp")
    item_count = tokens.shape[0]
    local_rows = tokens.shape[1]
    feature_shard = tokens.shape[2]
    feature_total = feature_shard * split_count
    head_width = input_weight.shape[3]
    head_count = head_width // HD
    norm_weight = lax.all_gather(input_weight[0][:, :2], "tp", axis=2, tiled=True).reshape(
        feature_total, 2 * head_width * split_count
    )
    joint_weight = jnp.concatenate([norm_weight, input_weight[0][:, 2]], axis=1)
    out_full = lax.all_gather(output_weight[0], "tp", axis=0, tiled=True)
    modulate_rows = modulation[0]
    norm_gains = norm_gain[0]
    local_number = jnp.arange(local_rows, dtype=jnp.int32)
    row_slots = patch_index * local_rows + local_number

    stale = heads_first(stale_cache[0])
    first_a = spread(stale[0], "sz", ring)
    first_b = spread(stale[1], "sy", rows_y)
    first_a, first_b, tokens = lax.optimization_barrier((first_a, first_b, tokens))
    stale_a = ring_gather(first_a, "sy")
    stale_b = ring_gather(first_b, "sz")

    y_offsets = jnp.arange(rows_y, dtype=jnp.int32)
    ring_offsets = jnp.arange(ring, dtype=jnp.int32)
    patch_a = ((row_y + y_offsets[:, None]) % rows_y) * ring + ring_offsets[None, :]
    patch_b = y_offsets[None, :] * ring + (row_z + ring_offsets[:, None]) % ring
    chosen_all = recompute[0].reshape(item_count, seq_count, RECOMP)
    own_chosen = lax.dynamic_slice_in_dim(chosen_all, patch_index, 1, axis=1)[:, 0]

    def stale_keep(patch_of):
        picks = jnp.take(chosen_all, patch_of.reshape(-1), axis=1).reshape(
            (item_count,) + patch_of.shape + (RECOMP,)
        )
        recomputed = jnp.any(local_number[:, None] == picks[..., None, :], axis=-1)
        slots = patch_of[..., None] * local_rows + local_number
        live = slots[None] < lengths[:, None, None, None]
        other = (patch_of != patch_index)[None, :, :, None]
        return (live & other & ~recomputed)[:, None]

    keep_a = stale_keep(patch_a)
    keep_b = stale_keep(patch_b)
    all_patches = jnp.arange(seq_count, dtype=jnp.int32)
    fresh_slots = all_patches[None, :, None] * local_rows + chosen_all
    keep_fresh = (
        (fresh_slots < lengths[:, None, None]) & (all_patches != patch_index)[None, :, None]
    )[:, None]
    keep_own = (row_slots[None, :] < lengths[:, None])[:, None]

    def layer(gathered):
        as_float = gathered.astype(jnp.float32)
        row_mean = jnp.mean(as_float, axis=-1, keepdims=True)
        centered = as_float - row_mean
        variance = jnp.mean(centered * centered, axis=-1, keepdims=True)
        modulated = (
            centered * lax.rsqrt(variance + 1e-06) * (1.0 + modulate_rows[1]) + modulate_rows[0]
        ).astype(jnp.bfloat16)
        projected = jnp.dot(modulated, joint_weight, preferred_element_type=jnp.float32)
        all_width = head_width * split_count
        every_head = projected[..., : 2 * all_width].reshape(item_count, local_rows, 2, all_width)
        square_total = jnp.moveaxis(jnp.sum(every_head * every_head, axis=-1), -1, 0)
        own_heads = lax.dynamic_slice_in_dim(every_head, split_index * head_width, head_width, axis=3)
        query_raw = own_heads[:, :, 0]
        key_raw = own_heads[:, :, 1]
        value_rows = projected[..., 2 * all_width :].astype(jnp.bfloat16)
        entry_total = head_width * split_count
        query_normed = (
            query_raw * lax.rsqrt(square_total[0] / entry_total + 1e-06)[..., None] * norm_gains[0]
        )
        key_normed = key_raw * lax.rsqrt(square_total[1] / entry_total + 1e-06)[..., None] * norm_gains[1]
        fresh_query = rotate(query_normed, positions[0], positions[1], positions[2]).astype(jnp.bfloat16)
        fresh_key = rotate(key_normed, positions[0], positions[1], positions[2]).astype(jnp.bfloat16)
        own_fresh = jnp.stack([fresh_key, value_rows], axis=1)
        picked = jnp.take_along_axis(
            own_fresh, own_chosen[:, None, :, None], axis=2
        )
        fresh_all = spread(heads_first(picked), ("sy", "sz"), seq_count)
        outs = []
        for head, stale_h in enumerate((stale_a, stale_b)):
            cols = slice(head * HD, (head + 1) * HD)
            keep_h = (keep_a, keep_b)[head]
            groups = (
                (stale_h[:, :, 0], stale_h[:, :, 1], keep_h, "iqd,abikd->iqabk", "iqabk,abikd->iqd"),
                (
                    fresh_all[:, head, 0],
                    fresh_all[:, head, 1],
                    keep_fresh,
                    "iqd,pird->iqpr",
                    "iqpr,pird->iqd",
                ),
                (fresh_key[..., cols], value_rows[..., cols], keep_own, "iqd,ikd->iqk", "iqk,ikd->iqd"),
            )
            outs.append(attend(fresh_query[..., cols], groups))
        attention = jnp.concatenate(outs, axis=-1).astype(jnp.bfloat16)
        all_heads = jnp.transpose(spread(attention, "tp", split_count), (1, 2, 0, 3)).reshape(
            item_count, local_rows, head_width * split_count
        )
        summed = jnp.dot(all_heads, out_full, preferred_element_type=jnp.float32)
        result = as_float + modulate_rows[2] * summed
        valid_rows = row_slots[None, :] < lengths[:, None]
        return jnp.where(valid_rows[..., None], result, 0.0).astype(jnp.bfloat16)

    whole_tokens = jnp.transpose(spread(tokens, "tp", split_count), (1, 2, 0, 3)).reshape(
        item_count, local_rows, feature_total
    )
    first = layer(whole_tokens)
    carried = lax.ppermute(first, "section", [(0, 1)])
    second = layer(carried)
    chosen_rows = jnp.where(section_index == 0, first, second)
    own_part = lax.dynamic_slice_in_dim(chosen_rows, split_index * feature_shard, feature_shard, axis=2)
    return own_part[None]


def solution(mesh):
    sizes = dict(mesh.shape)
    inner = 8
    devices = mesh.devices.reshape(sizes["section"], sizes["seq"] // inner, inner, sizes["tp"])
    mesh = Mesh(devices, ("section", "sy", "sz", "tp"))
    seq = ("sy", "sz")
    placed = (
        P(None, seq, "tp"),
        P("section", None, None, "tp"),
        P("section", "tp", None),
        P("section", None, None),
        P("section", None, "tp"),
        P("section", None, None, seq, "tp"),
        P("section", None, None),
        P(None, None, seq),
        P(),
    )
    return jax.shard_map(
        local,
        mesh=mesh,
        in_specs=placed,
        out_specs=P("section", None, seq, "tp"),
        check_vma=False,
    )
```

```python
import jax
import jax.numpy as jnp
from jax import lax
from jax.sharding import Mesh, PartitionSpec as P

HD = 128
RECOMP = 4


floor_score = -1e30


def ring_gather(block, axis):
    n = lax.axis_size(axis)
    plus = [(i, (i + 1) % n) for i in range(n)]
    minus = [(i, (i - 1) % n) for i in range(n)]
    rel = [None] * n
    rel[0] = block
    fwd = block
    bwd = block
    for step in range(1, n // 2):
        fwd = lax.ppermute(fwd, axis, plus)
        bwd = lax.ppermute(bwd, axis, minus)
        rel[n - step] = fwd
        rel[step] = bwd
    rel[n // 2] = lax.ppermute(fwd, axis, plus)
    return jnp.stack(rel)


def spread(x, axis, count):
    send = jnp.broadcast_to(x[None], (count,) + x.shape)
    return lax.all_to_all(send, axis, 0, 0)


def rotate(field_rows, frame_place, height_place, width_place):
    lead = field_rows.shape[:-1]
    pair_count = HD // 2
    side_pairs = pair_count // 3
    frame_pairs = pair_count - 2 * side_pairs

    def spacing(pair_total):
        ladder = jnp.arange(pair_total, dtype=jnp.float32)
        return jnp.power(jnp.float32(10000.0), -ladder / pair_total)

    angles = jnp.concatenate(
        [
            frame_place.astype(jnp.float32)[..., None] * spacing(frame_pairs),
            height_place.astype(jnp.float32)[..., None] * spacing(side_pairs),
            width_place.astype(jnp.float32)[..., None] * spacing(side_pairs),
        ],
        axis=-1,
    )
    cosine = jnp.cos(angles)[..., None, :]
    sine_part = jnp.sin(angles)[..., None, :]
    paired = field_rows.reshape(lead + (-1, pair_count, 2))
    first_half = paired[..., 0]
    second = paired[..., 1]
    turned = jnp.stack(
        [first_half * cosine - second * sine_part, first_half * sine_part + second * cosine],
        axis=-1,
    )
    return turned.reshape(lead + (-1,))


def attend(query, groups):
    scored = []
    for keys, values, keep, score_spec, value_spec in groups:
        scores = jnp.einsum(score_spec, query, keys, preferred_element_type=jnp.float32) * HD ** (-0.5)
        scores = jnp.where(keep, scores, floor_score)
        scored.append(scores)
    key_axes = [tuple(range(2, x.ndim)) for x in scored]
    top = scored[0].max(axis=key_axes[0])
    for scores, axes in zip(scored[1:], key_axes[1:]):
        top = jnp.maximum(top, scores.max(axis=axes))
    total = 0.0
    numerator = 0.0
    for scores, axes, (keys, values, keep, score_spec, value_spec) in zip(scored, key_axes, groups):
        top_b = top.reshape(top.shape + (1,) * len(axes))
        weights = jnp.where(keep, jnp.exp(scores - top_b), 0.0)
        total = total + jnp.sum(weights, axis=axes)
        numerator = numerator + jnp.einsum(
            value_spec, weights.astype(jnp.bfloat16), values, preferred_element_type=jnp.float32
        )
    return numerator / total[..., None]


def heads_first(x):
    lead = x.shape[:-1]
    return jnp.transpose(x.reshape(lead + (-1, HD)), (3, 1, 0, 2, 4))


def local(
    tokens,
    input_weight,
    output_weight,
    modulation,
    norm_gain,
    stale_cache,
    recompute,
    positions,
    lengths,
):
    section_index = lax.axis_index("section")
    ring = lax.axis_size("sz")
    rows_y = lax.axis_size("sy")
    seq_count = rows_y * ring
    row_y = lax.axis_index("sy")
    row_z = lax.axis_index("sz")
    patch_index = row_y * ring + row_z
    split_count = lax.axis_size("tp")
    split_index = lax.axis_index("tp")
    item_count = tokens.shape[0]
    local_rows = tokens.shape[1]
    feature_shard = tokens.shape[2]
    feature_total = feature_shard * split_count
    head_width = input_weight.shape[3]
    head_count = head_width // HD
    norm_weight = lax.all_gather(input_weight[0][:, :2], "tp", axis=2, tiled=True).reshape(
        feature_total, 2 * head_width * split_count
    )
    joint_weight = jnp.concatenate([norm_weight, input_weight[0][:, 2]], axis=1)
    out_full = lax.all_gather(output_weight[0], "tp", axis=0, tiled=True)
    modulate_rows = modulation[0]
    norm_gains = norm_gain[0]
    local_number = jnp.arange(local_rows, dtype=jnp.int32)
    row_slots = patch_index * local_rows + local_number

    stale = heads_first(stale_cache[0])
    first_a = spread(stale[0], "sz", ring)
    first_b = spread(stale[1], "sy", rows_y)
    whole_tokens = jnp.transpose(spread(tokens, "tp", split_count), (1, 2, 0, 3)).reshape(
        item_count, local_rows, feature_total
    )
    first_a, first_b, whole_tokens = lax.optimization_barrier((first_a, first_b, whole_tokens))
    stale_a = ring_gather(first_a, "sy")
    stale_b = ring_gather(first_b, "sz")

    y_offsets = jnp.arange(rows_y, dtype=jnp.int32)
    ring_offsets = jnp.arange(ring, dtype=jnp.int32)
    patch_a = ((row_y + y_offsets[:, None]) % rows_y) * ring + ring_offsets[None, :]
    patch_b = y_offsets[None, :] * ring + (row_z + ring_offsets[:, None]) % ring
    chosen_all = recompute[0].reshape(item_count, seq_count, RECOMP)
    own_chosen = lax.dynamic_slice_in_dim(chosen_all, patch_index, 1, axis=1)[:, 0]

    def stale_keep(patch_of):
        picks = jnp.take(chosen_all, patch_of.reshape(-1), axis=1).reshape(
            (item_count,) + patch_of.shape + (RECOMP,)
        )
        recomputed = jnp.any(local_number[:, None] == picks[..., None, :], axis=-1)
        slots = patch_of[..., None] * local_rows + local_number
        live = slots[None] < lengths[:, None, None, None]
        other = (patch_of != patch_index)[None, :, :, None]
        return (live & other & ~recomputed)[:, None]

    keep_a = stale_keep(patch_a)
    keep_b = stale_keep(patch_b)
    all_patches = jnp.arange(seq_count, dtype=jnp.int32)
    fresh_slots = all_patches[None, :, None] * local_rows + chosen_all
    keep_fresh = (
        (fresh_slots < lengths[:, None, None]) & (all_patches != patch_index)[None, :, None]
    )[:, None]
    keep_own = (row_slots[None, :] < lengths[:, None])[:, None]

    def layer(gathered):
        as_float = gathered.astype(jnp.float32)
        row_mean = jnp.mean(as_float, axis=-1, keepdims=True)
        centered = as_float - row_mean
        variance = jnp.mean(centered * centered, axis=-1, keepdims=True)
        modulated = (
            centered * lax.rsqrt(variance + 1e-06) * (1.0 + modulate_rows[1]) + modulate_rows[0]
        ).astype(jnp.bfloat16)
        projected = jnp.dot(modulated, joint_weight, preferred_element_type=jnp.float32)
        all_width = head_width * split_count
        every_head = projected[..., : 2 * all_width].reshape(item_count, local_rows, 2, all_width)
        square_total = jnp.moveaxis(jnp.sum(every_head * every_head, axis=-1), -1, 0)
        own_heads = lax.dynamic_slice_in_dim(every_head, split_index * head_width, head_width, axis=3)
        query_raw = own_heads[:, :, 0]
        key_raw = own_heads[:, :, 1]
        value_rows = projected[..., 2 * all_width :].astype(jnp.bfloat16)
        entry_total = head_width * split_count
        query_normed = (
            query_raw * lax.rsqrt(square_total[0] / entry_total + 1e-06)[..., None] * norm_gains[0]
        )
        key_normed = key_raw * lax.rsqrt(square_total[1] / entry_total + 1e-06)[..., None] * norm_gains[1]
        fresh_query = rotate(query_normed, positions[0], positions[1], positions[2]).astype(jnp.bfloat16)
        fresh_key = rotate(key_normed, positions[0], positions[1], positions[2]).astype(jnp.bfloat16)
        own_fresh = jnp.stack([fresh_key, value_rows], axis=1)
        picked = jnp.take_along_axis(
            own_fresh, own_chosen[:, None, :, None], axis=2
        )
        fresh_all = spread(heads_first(picked), ("sy", "sz"), seq_count)
        outs = []
        for head, stale_h in enumerate((stale_a, stale_b)):
            cols = slice(head * HD, (head + 1) * HD)
            keep_h = (keep_a, keep_b)[head]
            groups = (
                (stale_h[:, :, 0], stale_h[:, :, 1], keep_h, "iqd,abikd->iqabk", "iqabk,abikd->iqd"),
                (
                    fresh_all[:, head, 0],
                    fresh_all[:, head, 1],
                    keep_fresh,
                    "iqd,pird->iqpr",
                    "iqpr,pird->iqd",
                ),
                (fresh_key[..., cols], value_rows[..., cols], keep_own, "iqd,ikd->iqk", "iqk,ikd->iqd"),
            )
            outs.append(attend(fresh_query[..., cols], groups))
        attention = jnp.concatenate(outs, axis=-1).astype(jnp.bfloat16)
        all_heads = jnp.transpose(spread(attention, "tp", split_count), (1, 2, 0, 3)).reshape(
            item_count, local_rows, head_width * split_count
        )
        summed = jnp.dot(all_heads, out_full, preferred_element_type=jnp.float32)
        result = as_float + modulate_rows[2] * summed
        valid_rows = row_slots[None, :] < lengths[:, None]
        return jnp.where(valid_rows[..., None], result, 0.0).astype(jnp.bfloat16)

    first = layer(whole_tokens)
    carried = lax.ppermute(first, "section", [(0, 1)])
    second = layer(carried)
    chosen_rows = jnp.where(section_index == 0, first, second)
    own_part = lax.dynamic_slice_in_dim(chosen_rows, split_index * feature_shard, feature_shard, axis=2)
    return own_part[None]


def solution(mesh):
    sizes = dict(mesh.shape)
    inner = 8
    devices = mesh.devices.reshape(sizes["section"], sizes["seq"] // inner, inner, sizes["tp"])
    mesh = Mesh(devices, ("section", "sy", "sz", "tp"))
    seq = ("sy", "sz")
    placed = (
        P(None, seq, "tp"),
        P("section", None, None, "tp"),
        P("section", "tp", None),
        P("section", None, None),
        P("section", None, "tp"),
        P("section", None, None, seq, "tp"),
        P("section", None, None),
        P(None, None, seq),
        P(),
    )
    return jax.shard_map(
        local,
        mesh=mesh,
        in_specs=placed,
        out_specs=P("section", None, seq, "tp"),
        check_vma=False,
    )
```
